256 devices in a mesh: lat: 8 (over x, y_hi), lon: 8 (over z), lev: 4 (over y_lo, core).
Axes of the slice: x: 4, y: 4 (y_hi: 2, y_lo: 2; y = y_hi * 2 + y_lo), z: 8, core: 2. Of those that a mesh axis runs over, the one named last changes fastest.
Arguments:
- fields: float32 [3, 16, 1280, 3072], P(None, 'lev', 'lat', 'lon'), may hold values from -6 to 6
- sl_weights: float32 [40, 24, 128, 128], P('lat', 'lon'), may hold values from -0.5 to 0.5
- sl_tile: int32 [40, 24], P('lat', 'lon'), may hold values from -1 to 1
- daylit: int32 [1280, 24], P('lat', 'lon'), may hold values from 0 to 1, as said below
- absorption: float32 [32], replicated, may hold values from 0.05 to 5
- continuum: float32 [32], replicated, may hold values from 0.05 to 2
- albedo: float32 [32], replicated, may hold values from 0.5 to 0.95
- wave_ids: int32 [640], replicated, may hold values from 0 to 639, each once
- legendre: float32 [640, 640, 1280], P(('lat', 'lon'), 'lev'), may hold values from -0.15625 to 0.15625
Outputs:
- spectral: float32 [640, 2, 3, 16, 640], P(('lat', 'lon'), None, None, None, 'lev')
The draws below stay inside these ranges and needn't reach their ends.
Inputs may be any that keep to these rules, and one draw needn't show every extreme that they name: `daylit`: in every latitude row, at most one of the blocks b and b + 12 is sunlit. `wave_ids`: every wavenumber appears in exactly one slot.
All inputs are finite; a program needn't handle non-finite values.
Results may differ from the reference program's by a relative error of at most 0.000068.
Values sent between devices are 32-bit elements; how exact they have to be, the bound alone decides.
No kernel may reach another device: no remote copies, remote signals or barrier semaphores. Data moves between devices by JAX's collectives and lax.ppermute only.
A program may use at most 192 MiB of HBM per device.

```python
import math
import jax
import jax.numpy as jnp
from jax import lax

NLAT = 1280
NLON = 3072
MW = 640
F = 3
G = 32
TILE = 128
LATB = 32
LEV = 16


def draw_daylit(key, part):
    key_start, key_tilt, polar_key = jax.random.split(key, 3)
    segment_count = NLON // TILE
    row_ids = jnp.arange(NLAT, dtype=jnp.int32)
    sun_start = jax.random.randint(key_start, (), 0, segment_count)
    tilt_steps = jax.random.randint(key_tilt, (), 0, 4)
    polar_rows = jax.random.randint(polar_key, (), 0, NLAT // 8 + 1)
    sun_block = (sun_start + row_ids * tilt_steps * segment_count // (4 * NLAT)) % segment_count
    block_ids = jnp.arange(segment_count, dtype=jnp.int32)
    sunny = (block_ids[None, :] - sun_block[:, None]) % segment_count < segment_count // 2
    sunny = sunny & (row_ids[:, None] >= polar_rows)
    return sunny.astype(jnp.int32)


def place_ends(values, rng, low, top_value):
    shape = values.shape
    place = [jax.random.randint(jax.random.fold_in(rng, axis), (), 0, shape[axis]) for axis in range(len(shape))]
    values = values.at[tuple(place)].set(low)
    longest = shape.index(max(shape))
    place[longest] = (place[longest] + 1) % shape[longest]
    return values.at[tuple(place)].set(top_value)


def shard_levels(key, dims, cuts, smallest, top_value):
    factor_of = 1.0
    for position, shards_of in cuts:
        steps = jax.random.uniform(jax.random.fold_in(jax.random.fold_in(key, 6), position), (shards_of,), jnp.float32, smallest / len(cuts), top_value / len(cuts))
        factor_of = factor_of * jnp.repeat(jnp.exp(steps), dims[position] // shards_of).reshape((-1,) + (1,) * (len(dims) - 1 - position))
    return factor_of


def scatter_about(stream_key, dims, scale, reach, shards=(), held_as=jnp.bfloat16):
    result = scale * jax.random.normal(stream_key, dims, jnp.float32)
    if shards:
        result = result * shard_levels(stream_key, dims, shards, -0.22, 0.18)
    return jnp.clip(result, -reach, reach).astype(held_as)


def setup_inputs(seed: int = 0) -> dict:
    key_list = jax.random.split(jax.random.key(seed), 10)
    fields = scatter_about(key_list[0], (F, LEV, NLAT, NLON), 1.0, 6.0, ((1, 4), (2, 8), (3, 8)), jnp.float32)
    sl_weights = scatter_about(key_list[1], (NLAT // LATB, NLON // TILE, TILE, TILE), TILE ** -0.5, 0.5, ((0, 8), (1, 8)), jnp.float32)
    sl_tile = place_ends(jax.random.randint(key_list[2], (NLAT // LATB, NLON // TILE), -1, 2), jax.random.fold_in(key_list[2], 1), -1, 1).astype(jnp.int32)
    daylit = draw_daylit(jax.random.fold_in(key_list[9], 71), 0)
    absorption = jnp.clip(jnp.exp(jax.random.uniform(key_list[4], (G,), jnp.float32, math.log(0.05), math.log(5.0))), 0.05, 5.0)
    continuum = jnp.clip(jnp.exp(jax.random.uniform(key_list[5], (G,), jnp.float32, math.log(0.05), math.log(2.0))), 0.05, 2.0)
    albedo = jnp.clip(jax.random.uniform(key_list[6], (G,), jnp.float32, 0.5, 0.95), 0.5, 0.95)
    wave_ids = jax.random.permutation(key_list[7], MW).astype(jnp.int32)
    legendre = scatter_about(key_list[8], (MW, MW, NLAT), NLAT ** -0.5, 0.15625, ((0, 64), (1, 4)), jnp.float32)
    return {"fields": fields, "sl_weights": sl_weights, "sl_tile": sl_tile, "daylit": daylit, "absorption": absorption, "continuum": continuum, "albedo": albedo, "wave_ids": wave_ids, "legendre": legendre}


highest = lax.Precision.HIGHEST
heat_rate = 6.0
asymmetry = 0.6

def absorbed_per_band(depth_wet, hot_extinction_thickness, above_wet, above_warm, absorb_part, continuum_part, reflectivity_share):
    gamma_one = (7.0 - reflectivity_share * (4.0 + 3.0 * asymmetry)) / 4.0
    gamma_two = -(1.0 - reflectivity_share * (4.0 - 3.0 * asymmetry)) / 4.0
    eigen_rate = jnp.sqrt(gamma_one * gamma_one - gamma_two * gamma_two)
    optical = absorb_part * depth_wet + continuum_part * hot_extinction_thickness
    beam = jnp.exp(-(absorb_part * above_wet + continuum_part * above_warm))
    decay = jnp.exp(-eigen_rate * optical)
    decay_sq = decay * decay
    denominator = eigen_rate + gamma_one + (eigen_rate - gamma_one) * decay_sq
    reflect = gamma_two * (1.0 - decay_sq) / denominator
    transmit = 2.0 * eigen_rate * decay / denominator
    return beam * (1.0 - reflect - transmit)

def reference(fields, sl_weights, sl_tile, daylit, absorption, continuum, albedo, wave_ids, legendre):
    row_blocks = NLAT // LATB
    tile_count = NLON // TILE
    tile_rows = fields.reshape(F, LEV, row_blocks, LATB, tile_count, TILE)
    source_ids = (jnp.arange(tile_count, dtype=jnp.int32)[None, :] + sl_tile) % tile_count
    onehot = (source_ids[:, :, None] == jnp.arange(tile_count, dtype=jnp.int32)[None, None, :]).astype(jnp.float32)
    sources = jnp.einsum('flbrkc,bjk->flbrjc', tile_rows, onehot, precision=highest)
    departure_estimate = jnp.einsum('flbrjc,bjtc->flbrjt', sources, sl_weights, precision=highest).reshape(F, LEV, NLAT, NLON)
    moisture = departure_estimate[2]
    thermal_state = departure_estimate[0]
    stratum_factor = 4.0 / LEV
    depth_wet = stratum_factor * (0.2 + moisture * moisture)
    hot_extinction_thickness = stratum_factor * (0.2 + thermal_state * thermal_state)
    above_wet = jnp.concatenate([jnp.zeros_like(depth_wet[:1]), jnp.cumsum(depth_wet[:-1], axis=0)], axis=0)
    above_warm = jnp.concatenate([jnp.zeros_like(hot_extinction_thickness[:1]), jnp.cumsum(hot_extinction_thickness[:-1], axis=0)], axis=0)

    def add_band(band, running):
        return running + absorbed_per_band(depth_wet, hot_extinction_thickness, above_wet, above_warm, absorption[band], continuum[band], albedo[band])
    absorbed = lax.fori_loop(0, G, add_band, jnp.zeros_like(moisture)) / G
    sunlit = jnp.repeat(daylit.astype(jnp.float32), TILE, axis=1)
    heating = absorbed * sunlit[None]
    updated = jnp.concatenate([departure_estimate[:1] + heat_rate * heating[None], departure_estimate[1:]], axis=0)
    phases = wave_ids[:, None] * jnp.arange(NLON, dtype=jnp.int32)[None, :] % NLON
    angles = phases.astype(jnp.float32) * (2.0 * math.pi / NLON)
    dft_table = (jnp.stack([jnp.cos(angles), -jnp.sin(angles)], axis=1) / math.sqrt(NLON)).reshape(2 * MW, NLON)
    fourier = jnp.einsum('wn,flpn->wflp', dft_table, updated, precision=highest).reshape(MW, 2, F, LEV, NLAT)
    spectra = jnp.einsum('mcfls,mns->mcfln', fourier, legendre, precision=highest)
    keep_mask = jnp.arange(MW, dtype=jnp.int32)[None, :] >= wave_ids[:, None]
    return jnp.where(keep_mask[:, None, None, None, :], spectra, 0.0)
```

```python
import math

import jax
import jax.numpy as jnp
from jax import lax
from jax.sharding import PartitionSpec as P

highest = lax.Precision.HIGHEST
heat_rate = 6.0
asymmetry = 0.6


def with_halo(block, sides, width):
    for axis, dim in sides:
        count = lax.axis_size(axis)
        forward = [(i, i + 1) for i in range(count - 1)]
        forward.append((count - 1, 0))
        backward = [(target, source) for source, target in forward]
        low = lax.ppermute(
            lax.slice_in_dim(block, block.shape[dim] - width, None, axis=dim), axis, forward
        )
        high = lax.ppermute(lax.slice_in_dim(block, 0, width, axis=dim), axis, backward)
        block = jnp.concatenate([low, block, high], axis=dim)
    return block


def carried_in(planes, axis):
    mine = lax.axis_index(axis)
    pieces = lax.all_gather(planes, axis)
    count = pieces.shape[0]
    below = (jnp.arange(count, dtype=jnp.int32) < mine).reshape((count,) + (1,) * planes.ndim)
    return jnp.sum(jnp.where(below, pieces, 0.0), axis=0)


def absorbed_per_band(
    depth_wet,
    hot_extinction_thickness,
    above_wet,
    above_warm,
    absorb_part,
    continuum_part,
    reflectivity_share,
):
    gamma_one = (7.0 - reflectivity_share * (4.0 + 3.0 * asymmetry)) / 4.0
    gamma_two = -(1.0 - reflectivity_share * (4.0 - 3.0 * asymmetry)) / 4.0
    eigen_rate = jnp.sqrt(gamma_one * gamma_one - gamma_two * gamma_two)
    optical = absorb_part * depth_wet + continuum_part * hot_extinction_thickness
    beam = jnp.exp(-(absorb_part * above_wet + continuum_part * above_warm))
    decay = jnp.exp(-eigen_rate * optical)
    decay_sq = decay * decay
    denominator = eigen_rate + gamma_one + (eigen_rate - gamma_one) * decay_sq
    lost = (gamma_two * (1.0 - decay_sq) + 2.0 * eigen_rate * decay) / denominator
    return beam * (1.0 - lost)


def absorbed_mean(
    depth_wet, hot_extinction_thickness, above_wet, above_warm, absorption, continuum, albedo
):
    band_total = absorption.shape[0]
    band_group = min(8, band_total)
    unit_shape = (1,) * depth_wet.ndim
    running = jnp.zeros_like(depth_wet)
    for band_start in range(0, band_total, band_group):
        absorb_part = absorption[band_start : band_start + band_group].reshape(
            (band_group,) + unit_shape
        )
        continuum_part = continuum[band_start : band_start + band_group].reshape(
            (band_group,) + unit_shape
        )
        reflectivity_share = albedo[band_start : band_start + band_group].reshape(
            (band_group,) + unit_shape
        )
        terms = absorbed_per_band(
            depth_wet[None],
            hot_extinction_thickness[None],
            above_wet[None],
            above_warm[None],
            absorb_part,
            continuum_part,
            reflectivity_share,
        )
        running = running + jnp.sum(terms, axis=0)
    return running / band_total


def local(fields, sl_weights, sl_tile, daylit, absorption, continuum, albedo, wave_ids, legendre):
    meridian_number = lax.axis_size("lon")
    lat_count = lax.axis_size("lat")
    lev_count = lax.axis_size("lev")
    wave_devices = lat_count * meridian_number
    field_count, lev_local, lat_local, lon_local = fields.shape
    tile_width = sl_weights.shape[-1]
    tile_count = lon_local // tile_width
    row_blocks = sl_tile.shape[0]
    block_rows = lat_local // row_blocks
    padded = with_halo(fields, (("lon", 3),), tile_width)
    tile_rows = padded.reshape(
        field_count, lev_local, row_blocks, block_rows, tile_count + 2, tile_width
    )
    source_ids = jnp.arange(tile_count, dtype=jnp.int32)[None, :] + 1 + sl_tile
    onehot = (
        source_ids[:, :, None] == jnp.arange(tile_count + 2, dtype=jnp.int32)[None, None, :]
    ).astype(jnp.float32)
    sources = jnp.einsum("flbrkc,bjk->flbrjc", tile_rows, onehot, precision=highest)
    departure_estimate = jnp.einsum("flbrjc,bjtc->flbrjt", sources, sl_weights, precision=highest)
    departure_estimate = departure_estimate.reshape(field_count, lev_local, lat_local, lon_local)
    moisture = departure_estimate[2]
    thermal_state = departure_estimate[0]
    stratum_factor = 4.0 / (lev_local * lev_count)
    depth_wet = stratum_factor * (0.2 + moisture * moisture)
    hot_extinction_thickness = stratum_factor * (0.2 + thermal_state * thermal_state)
    prefix = carried_in(
        jnp.stack([jnp.sum(depth_wet, axis=0), jnp.sum(hot_extinction_thickness, axis=0)]), "lev"
    )
    prefix_wet, prefix_warm = prefix[0], prefix[1]
    wet_levels = []
    warm_levels = []
    for level in range(lev_local):
        wet_levels.append(prefix_wet)
        warm_levels.append(prefix_warm)
        prefix_wet = prefix_wet + depth_wet[level]
        prefix_warm = prefix_warm + hot_extinction_thickness[level]
    above_wet = jnp.stack(wet_levels, axis=0)
    above_warm = jnp.stack(warm_levels, axis=0)
    absorbed = absorbed_mean(
        depth_wet, hot_extinction_thickness, above_wet, above_warm, absorption, continuum, albedo
    )
    absorbed = absorbed.reshape(lev_local, lat_local, tile_count, tile_width)
    heating = (absorbed * daylit.astype(jnp.float32)[None, :, :, None]).reshape(
        lev_local, lat_local, lon_local
    )
    updated = jnp.concatenate(
        [departure_estimate[:1] + heat_rate * heating[None], departure_estimate[1:]], axis=0
    )
    rows_each = lat_local // meridian_number
    mesh_lines = updated.reshape(field_count, lev_local, meridian_number, rows_each, lon_local)
    sectors = lax.all_to_all(mesh_lines, "lon", split_axis=2, concat_axis=2, tiled=True)
    lon_total = lon_local * meridian_number
    wave_total = wave_ids.shape[0]
    inner = jnp.arange(lon_local, dtype=jnp.int32)
    phases = wave_ids[:, None] * inner[None, :] % lon_total
    angles = phases.astype(jnp.float32) * (2.0 * math.pi / lon_total)
    scale = 1.0 / math.sqrt(lon_total)
    dft_table = jnp.concatenate([jnp.cos(angles) * scale, jnp.sin(angles) * scale], axis=0)
    partial = jnp.einsum("wn,fldrn->wdflr", dft_table, sectors, precision=highest)
    partial = partial.reshape(2, wave_total, meridian_number, field_count, lev_local, rows_each)
    turns = wave_ids[:, None] * jnp.arange(meridian_number, dtype=jnp.int32)[None, :] % meridian_number
    turn_angles = turns.astype(jnp.float32) * (2.0 * math.pi / meridian_number)
    turn_cos = jnp.cos(turn_angles)[:, :, None, None, None]
    turn_sin = jnp.sin(turn_angles)[:, :, None, None, None]
    real_part = jnp.sum(turn_cos * partial[0] - turn_sin * partial[1], axis=1)
    imag_part = -jnp.sum(turn_sin * partial[0] + turn_cos * partial[1], axis=1)
    fourier = jnp.stack([real_part, imag_part], axis=1)
    waves_local = wave_total // wave_devices
    outgoing_waves = fourier.reshape(
        wave_devices, 2 * waves_local, field_count, lev_local, 1, rows_each
    )
    arrived = lax.all_to_all(
        outgoing_waves, ("lat", "lon"), split_axis=0, concat_axis=4, tiled=True
    )
    spectral_in = arrived.reshape(waves_local, 2, field_count, lev_local, wave_devices * rows_each)
    spectra = jnp.einsum(
        "mcfls,mns->mcfln",
        lax.all_gather(spectral_in, "lev", axis=3, tiled=True),
        legendre,
        precision=highest,
    )
    degree_local = legendre.shape[1]
    degrees = lax.axis_index("lev") * degree_local + jnp.arange(degree_local, dtype=jnp.int32)
    own_waves = lax.dynamic_slice_in_dim(
        wave_ids, lax.axis_index(("lat", "lon")) * waves_local, waves_local
    )
    keep_mask = degrees[None, :] >= own_waves[:, None]
    return jnp.where(keep_mask[:, None, None, None, :], spectra, 0.0)


def solution(mesh):
    in_specs = (
        P(None, "lev", "lat", "lon"),
        P("lat", "lon", None, None),
        P("lat", "lon"),
        P("lat", "lon"),
        P(),
        P(),
        P(),
        P(),
        P(("lat", "lon"), "lev", None),
    )
    out_specs = P(("lat", "lon"), None, None, None, "lev")
    return jax.shard_map(local, mesh=mesh, in_specs=in_specs, out_specs=out_specs, check_vma=False)
```

```python
import math

import jax
import jax.numpy as jnp
from jax import lax
from jax.sharding import PartitionSpec as P

highest = lax.Precision.HIGHEST
heat_rate = 6.0
asymmetry = 0.6


def with_halo(block, sides, width):
    for axis, dim in sides:
        count = lax.axis_size(axis)
        forward = [(i, i + 1) for i in range(count - 1)]
        forward.append((count - 1, 0))
        backward = [(target, source) for source, target in forward]
        low = lax.ppermute(
            lax.slice_in_dim(block, block.shape[dim] - width, None, axis=dim), axis, forward
        )
        high = lax.ppermute(lax.slice_in_dim(block, 0, width, axis=dim), axis, backward)
        block = jnp.concatenate([low, block, high], axis=dim)
    return block


def carried_in(planes, axis):
    mine = lax.axis_index(axis)
    pieces = lax.all_gather(planes, axis)
    count = pieces.shape[0]
    below = (jnp.arange(count, dtype=jnp.int32) < mine).reshape((count,) + (1,) * planes.ndim)
    return jnp.sum(jnp.where(below, pieces, 0.0), axis=0)


def absorbed_per_band(
    depth_wet,
    hot_extinction_thickness,
    above_wet,
    above_warm,
    absorb_part,
    continuum_part,
    reflectivity_share,
):
    gamma_one = (7.0 - reflectivity_share * (4.0 + 3.0 * asymmetry)) / 4.0
    gamma_two = -(1.0 - reflectivity_share * (4.0 - 3.0 * asymmetry)) / 4.0
    eigen_rate = jnp.sqrt(gamma_one * gamma_one - gamma_two * gamma_two)
    optical = absorb_part * depth_wet + continuum_part * hot_extinction_thickness
    beam = jnp.exp(-(absorb_part * above_wet + continuum_part * above_warm))
    decay = jnp.exp(-eigen_rate * optical)
    decay_sq = decay * decay
    denominator = eigen_rate + gamma_one + (eigen_rate - gamma_one) * decay_sq
    lost = (gamma_two * (1.0 - decay_sq) + 2.0 * eigen_rate * decay) / denominator
    return beam * (1.0 - lost)


def absorbed_mean(
    depth_wet, hot_extinction_thickness, above_wet, above_warm, absorption, continuum, albedo
):
    band_total = absorption.shape[0]
    band_group = min(8, band_total)
    unit_shape = (1,) * depth_wet.ndim
    running = jnp.zeros_like(depth_wet)
    for band_start in range(0, band_total, band_group):
        absorb_part = absorption[band_start : band_start + band_group].reshape(
            (band_group,) + unit_shape
        )
        continuum_part = continuum[band_start : band_start + band_group].reshape(
            (band_group,) + unit_shape
        )
        reflectivity_share = albedo[band_start : band_start + band_group].reshape(
            (band_group,) + unit_shape
        )
        terms = absorbed_per_band(
            depth_wet[None],
            hot_extinction_thickness[None],
            above_wet[None],
            above_warm[None],
            absorb_part,
            continuum_part,
            reflectivity_share,
        )
        running = running + jnp.sum(terms, axis=0)
    return running / band_total


def local(fields, sl_weights, sl_tile, daylit, absorption, continuum, albedo, wave_ids, legendre):
    meridian_number = lax.axis_size("lon")
    lat_count = lax.axis_size("lat")
    lev_count = lax.axis_size("lev")
    wave_devices = lat_count * meridian_number
    field_count, lev_local, lat_local, lon_local = fields.shape
    tile_width = sl_weights.shape[-1]
    tile_count = lon_local // tile_width
    row_blocks = sl_tile.shape[0]
    block_rows = lat_local // row_blocks
    padded = with_halo(fields, (("lon", 3),), tile_width)
    tile_rows = padded.reshape(
        field_count, lev_local, row_blocks, block_rows, tile_count + 2, tile_width
    )
    source_ids = jnp.arange(tile_count, dtype=jnp.int32)[None, :] + 1 + sl_tile
    onehot = (
        source_ids[:, :, None] == jnp.arange(tile_count + 2, dtype=jnp.int32)[None, None, :]
    ).astype(jnp.float32)
    sources = jnp.einsum("flbrkc,bjk->flbrjc", tile_rows, onehot, precision=highest)
    departure_estimate = jnp.einsum("flbrjc,bjtc->flbrjt", sources, sl_weights, precision=highest)
    departure_estimate = departure_estimate.reshape(field_count, lev_local, lat_local, lon_local)
    moisture = departure_estimate[2]
    thermal_state = departure_estimate[0]
    stratum_factor = 4.0 / (lev_local * lev_count)
    depth_wet = stratum_factor * (0.2 + moisture * moisture)
    hot_extinction_thickness = stratum_factor * (0.2 + thermal_state * thermal_state)
    prefix = carried_in(
        jnp.stack([jnp.sum(depth_wet, axis=0), jnp.sum(hot_extinction_thickness, axis=0)]), "lev"
    )
    prefix_wet, prefix_warm = prefix[0], prefix[1]
    wet_levels = []
    warm_levels = []
    for level in range(lev_local):
        wet_levels.append(prefix_wet)
        warm_levels.append(prefix_warm)
        prefix_wet = prefix_wet + depth_wet[level]
        prefix_warm = prefix_warm + hot_extinction_thickness[level]
    above_wet = jnp.stack(wet_levels, axis=0)
    above_warm = jnp.stack(warm_levels, axis=0)
    absorbed = absorbed_mean(
        depth_wet, hot_extinction_thickness, above_wet, above_warm, absorption, continuum, albedo
    )
    absorbed = absorbed.reshape(lev_local, lat_local, tile_count, tile_width)
    heating = (absorbed * daylit.astype(jnp.float32)[None, :, :, None]).reshape(
        lev_local, lat_local, lon_local
    )
    rows_each = lat_local // meridian_number

    def to_sectors(block):
        lines = block.reshape(block.shape[0], lev_local, meridian_number, rows_each, lon_local)
        return lax.all_to_all(lines, "lon", split_axis=2, concat_axis=2, tiled=True)

    sectors_rest = to_sectors(departure_estimate[1:])
    sectors_heat = to_sectors(departure_estimate[:1] + heat_rate * heating[None])
    lon_total = lon_local * meridian_number
    wave_total = wave_ids.shape[0]
    inner = jnp.arange(lon_local, dtype=jnp.int32)
    phases = wave_ids[:, None] * inner[None, :] % lon_total
    angles = phases.astype(jnp.float32) * (2.0 * math.pi / lon_total)
    scale = 1.0 / math.sqrt(lon_total)
    dft_table = jnp.concatenate([jnp.cos(angles) * scale, jnp.sin(angles) * scale], axis=0)
    turns = wave_ids[None, :] * jnp.arange(meridian_number, dtype=jnp.int32)[:, None] % meridian_number
    turn_angles = turns.astype(jnp.float32) * (2.0 * math.pi / meridian_number)
    turn_cos = jnp.cos(turn_angles)[:, :, None]
    turn_sin = jnp.sin(turn_angles)[:, :, None]

    def transform(sectors):
        partial = jnp.einsum("wn,fldrn->dwflr", dft_table, sectors, precision=highest)
        partial = partial.reshape(meridian_number, 2, wave_total, -1)
        real_part = jnp.sum(turn_cos * partial[:, 0] - turn_sin * partial[:, 1], axis=0)
        imag_part = -jnp.sum(turn_sin * partial[:, 0] + turn_cos * partial[:, 1], axis=0)
        return jnp.stack([real_part, imag_part], axis=1)

    fourier = jnp.concatenate([transform(sectors_heat), transform(sectors_rest)], axis=-1)
    waves_local = wave_total // wave_devices
    row_total = field_count * lev_local * rows_each
    outgoing_waves = fourier.reshape(wave_devices, 2 * waves_local, row_total)
    arrived = lax.all_to_all(
        outgoing_waves, ("lat", "lon"), split_axis=0, concat_axis=0, tiled=True
    )
    arrived = arrived.reshape(wave_devices, waves_local, 2, field_count, lev_local, rows_each)
    spectral_in = arrived.transpose(1, 2, 3, 4, 0, 5).reshape(
        waves_local, 2, field_count, lev_local, wave_devices * rows_each
    )
    spectra = jnp.einsum(
        "mcfls,mns->mcfln",
        lax.all_gather(spectral_in, "lev", axis=3, tiled=True),
        legendre,
        precision=highest,
    )
    degree_local = legendre.shape[1]
    degrees = lax.axis_index("lev") * degree_local + jnp.arange(degree_local, dtype=jnp.int32)
    own_waves = lax.dynamic_slice_in_dim(
        wave_ids, lax.axis_index(("lat", "lon")) * waves_local, waves_local
    )
    keep_mask = degrees[None, :] >= own_waves[:, None]
    return jnp.where(keep_mask[:, None, None, None, :], spectra, 0.0)


def solution(mesh):
    in_specs = (
        P(None, "lev", "lat", "lon"),
        P("lat", "lon", None, None),
        P("lat", "lon"),
        P("lat", "lon"),
        P(),
        P(),
        P(),
        P(),
        P(("lat", "lon"), "lev", None),
    )
    out_specs = P(("lat", "lon"), None, None, None, "lev")
    return jax.shard_map(local, mesh=mesh, in_specs=in_specs, out_specs=out_specs, check_vma=False)
```

```python
import math

import jax
import jax.numpy as jnp
from jax import lax
from jax.sharding import PartitionSpec as P

highest = lax.Precision.HIGHEST
heat_rate = 6.0
asymmetry = 0.6


def with_halo(block, sides, width):
    for axis, dim in sides:
        count = lax.axis_size(axis)
        forward = [(i, i + 1) for i in range(count - 1)]
        forward.append((count - 1, 0))
        backward = [(target, source) for source, target in forward]
        low = lax.ppermute(
            lax.slice_in_dim(block, block.shape[dim] - width, None, axis=dim), axis, forward
        )
        high = lax.ppermute(lax.slice_in_dim(block, 0, width, axis=dim), axis, backward)
        block = jnp.concatenate([low, block, high], axis=dim)
    return block


def carried_in(planes, axis):
    mine = lax.axis_index(axis)
    pieces = lax.all_gather(planes, axis)
    count = pieces.shape[0]
    below = (jnp.arange(count, dtype=jnp.int32) < mine).reshape((count,) + (1,) * planes.ndim)
    return jnp.sum(jnp.where(below, pieces, 0.0), axis=0)


def absorbed_per_band(
    depth_wet,
    hot_extinction_thickness,
    above_wet,
    above_warm,
    absorb_part,
    continuum_part,
    reflectivity_share,
):
    gamma_one = (7.0 - reflectivity_share * (4.0 + 3.0 * asymmetry)) / 4.0
    gamma_two = -(1.0 - reflectivity_share * (4.0 - 3.0 * asymmetry)) / 4.0
    eigen_rate = jnp.sqrt(gamma_one * gamma_one - gamma_two * gamma_two)
    optical = absorb_part * depth_wet + continuum_part * hot_extinction_thickness
    beam = jnp.exp(-(absorb_part * above_wet + continuum_part * above_warm))
    decay = jnp.exp(-eigen_rate * optical)
    decay_sq = decay * decay
    denominator = eigen_rate + gamma_one + (eigen_rate - gamma_one) * decay_sq
    lost = (gamma_two * (1.0 - decay_sq) + 2.0 * eigen_rate * decay) / denominator
    return beam * (1.0 - lost)


def absorbed_mean(
    depth_wet, hot_extinction_thickness, above_wet, above_warm, absorption, continuum, albedo
):
    band_total = absorption.shape[0]
    band_group = min(8, band_total)
    unit_shape = (1,) * depth_wet.ndim
    running = jnp.zeros_like(depth_wet)
    for band_start in range(0, band_total, band_group):
        absorb_part = absorption[band_start : band_start + band_group].reshape(
            (band_group,) + unit_shape
        )
        continuum_part = continuum[band_start : band_start + band_group].reshape(
            (band_group,) + unit_shape
        )
        reflectivity_share = albedo[band_start : band_start + band_group].reshape(
            (band_group,) + unit_shape
        )
        terms = absorbed_per_band(
            depth_wet[None],
            hot_extinction_thickness[None],
            above_wet[None],
            above_warm[None],
            absorb_part,
            continuum_part,
            reflectivity_share,
        )
        running = running + jnp.sum(terms, axis=0)
    return running / band_total


def local(fields, sl_weights, sl_tile, daylit, absorption, continuum, albedo, wave_ids, legendre):
    meridian_number = lax.axis_size("lon")
    lat_count = lax.axis_size("lat")
    lev_count = lax.axis_size("lev")
    wave_devices = lat_count * meridian_number
    field_count, lev_local, lat_local, lon_local = fields.shape
    tile_width = sl_weights.shape[-1]
    tile_count = lon_local // tile_width
    row_blocks = sl_tile.shape[0]
    block_rows = lat_local // row_blocks
    padded = with_halo(fields, (("lon", 3),), tile_width)
    tile_rows = padded.reshape(
        field_count, lev_local, row_blocks, block_rows, tile_count + 2, tile_width
    )
    source_ids = jnp.arange(tile_count, dtype=jnp.int32)[None, :] + 1 + sl_tile
    onehot = (
        source_ids[:, :, None] == jnp.arange(tile_count + 2, dtype=jnp.int32)[None, None, :]
    ).astype(jnp.float32)
    sources = jnp.einsum("flbrkc,bjk->flbrjc", tile_rows, onehot, precision=highest)
    departure_estimate = jnp.einsum("flbrjc,bjtc->flbrjt", sources, sl_weights, precision=highest)
    departure_estimate = departure_estimate.reshape(field_count, lev_local, lat_local, lon_local)
    moisture = departure_estimate[2]
    thermal_state = departure_estimate[0]
    stratum_factor = 4.0 / (lev_local * lev_count)
    depth_wet = stratum_factor * (0.2 + moisture * moisture)
    hot_extinction_thickness = stratum_factor * (0.2 + thermal_state * thermal_state)
    prefix = carried_in(
        jnp.stack([jnp.sum(depth_wet, axis=0), jnp.sum(hot_extinction_thickness, axis=0)]), "lev"
    )
    prefix_wet, prefix_warm = prefix[0], prefix[1]
    wet_levels = []
    warm_levels = []
    for level in range(lev_local):
        wet_levels.append(prefix_wet)
        warm_levels.append(prefix_warm)
        prefix_wet = prefix_wet + depth_wet[level]
        prefix_warm = prefix_warm + hot_extinction_thickness[level]
    above_wet = jnp.stack(wet_levels, axis=0)
    above_warm = jnp.stack(warm_levels, axis=0)
    absorbed = absorbed_mean(
        depth_wet, hot_extinction_thickness, above_wet, above_warm, absorption, continuum, albedo
    )
    absorbed = absorbed.reshape(lev_local, lat_local, tile_count, tile_width)
    heating = (absorbed * daylit.astype(jnp.float32)[None, :, :, None]).reshape(
        lev_local, lat_local, lon_local
    )
    rows_each = lat_local // meridian_number

    def to_sectors(block):
        lines = block.reshape(block.shape[0], lev_local, meridian_number, rows_each, lon_local)
        return lax.all_to_all(lines, "lon", split_axis=2, concat_axis=2, tiled=True)

    sectors_rest = to_sectors(departure_estimate[1:])
    sectors_heat = to_sectors(departure_estimate[:1] + heat_rate * heating[None])
    lon_total = lon_local * meridian_number
    wave_total = wave_ids.shape[0]
    inner = jnp.arange(lon_local, dtype=jnp.int32)
    phases = wave_ids[:, None] * inner[None, :] % lon_total
    angles = phases.astype(jnp.float32) * (2.0 * math.pi / lon_total)
    scale = 1.0 / math.sqrt(lon_total)
    dft_table = jnp.concatenate([jnp.cos(angles) * scale, jnp.sin(angles) * scale], axis=0)
    turns = wave_ids[None, :] * jnp.arange(meridian_number, dtype=jnp.int32)[:, None] % meridian_number
    turn_angles = turns.astype(jnp.float32) * (2.0 * math.pi / meridian_number)
    turn_cos = jnp.cos(turn_angles)[:, :, None]
    turn_sin = jnp.sin(turn_angles)[:, :, None]

    def transform(sectors):
        partial = jnp.einsum("wn,fldrn->dwflr", dft_table, sectors, precision=highest)
        partial = partial.reshape(meridian_number, 2, wave_total, -1)
        real_part = jnp.sum(turn_cos * partial[:, 0] - turn_sin * partial[:, 1], axis=0)
        imag_part = -jnp.sum(turn_sin * partial[:, 0] + turn_cos * partial[:, 1], axis=0)
        return jnp.stack([real_part, imag_part], axis=1)

    waves_local = wave_total // wave_devices

    def analyse(sectors):
        chunk_fields = sectors.shape[0]
        fourier = transform(sectors)
        outgoing_waves = fourier.reshape(wave_devices, 2 * waves_local, -1)
        arrived = lax.all_to_all(
            outgoing_waves, ("lat", "lon"), split_axis=0, concat_axis=0, tiled=True
        )
        arrived = arrived.reshape(
            wave_devices, waves_local, 2, chunk_fields, lev_local, rows_each
        )
        spectral_in = arrived.transpose(1, 2, 3, 4, 0, 5).reshape(
            waves_local, 2, chunk_fields, lev_local, wave_devices * rows_each
        )
        return jnp.einsum(
            "mcfls,mns->mcfln",
            lax.all_gather(spectral_in, "lev", axis=3, tiled=True),
            legendre,
            precision=highest,
        )

    spectra = jnp.concatenate(
        [analyse(sectors_heat), analyse(sectors_rest[:1]), analyse(sectors_rest[1:])], axis=2
    )
    degree_local = legendre.shape[1]
    degrees = lax.axis_index("lev") * degree_local + jnp.arange(degree_local, dtype=jnp.int32)
    own_waves = lax.dynamic_slice_in_dim(
        wave_ids, lax.axis_index(("lat", "lon")) * waves_local, waves_local
    )
    keep_mask = degrees[None, :] >= own_waves[:, None]
    return jnp.where(keep_mask[:, None, None, None, :], spectra, 0.0)


def solution(mesh):
    in_specs = (
        P(None, "lev", "lat", "lon"),
        P("lat", "lon", None, None),
        P("lat", "lon"),
        P("lat", "lon"),
        P(),
        P(),
        P(),
        P(),
        P(("lat", "lon"), "lev", None),
    )
    out_specs = P(("lat", "lon"), None, None, None, "lev")
    return jax.shard_map(local, mesh=mesh, in_specs=in_specs, out_specs=out_specs, check_vma=False)
```

```python
import math

import jax
import jax.numpy as jnp
from jax import lax
from jax.sharding import PartitionSpec as P

highest = lax.Precision.HIGHEST
heat_rate = 6.0
asymmetry = 0.6


def with_halo(block, sides, width):
    for axis, dim in sides:
        count = lax.axis_size(axis)
        forward = [(i, i + 1) for i in range(count - 1)]
        forward.append((count - 1, 0))
        backward = [(target, source) for source, target in forward]
        low = lax.ppermute(
            lax.slice_in_dim(block, block.shape[dim] - width, None, axis=dim), axis, forward
        )
        high = lax.ppermute(lax.slice_in_dim(block, 0, width, axis=dim), axis, backward)
        block = jnp.concatenate([low, block, high], axis=dim)
    return block


def carried_in(planes, axis):
    mine = lax.axis_index(axis)
    pieces = lax.all_gather(planes, axis)
    count = pieces.shape[0]
    below = (jnp.arange(count, dtype=jnp.int32) < mine).reshape((count,) + (1,) * planes.ndim)
    return jnp.sum(jnp.where(below, pieces, 0.0), axis=0)


def absorbed_per_band(
    depth_wet,
    hot_extinction_thickness,
    above_wet,
    above_warm,
    absorb_part,
    continuum_part,
    reflectivity_share,
):
    gamma_one = (7.0 - reflectivity_share * (4.0 + 3.0 * asymmetry)) / 4.0
    gamma_two = -(1.0 - reflectivity_share * (4.0 - 3.0 * asymmetry)) / 4.0
    eigen_rate = jnp.sqrt(gamma_one * gamma_one - gamma_two * gamma_two)
    optical = absorb_part * depth_wet + continuum_part * hot_extinction_thickness
    beam = jnp.exp(-(absorb_part * above_wet + continuum_part * above_warm))
    decay = jnp.exp(-eigen_rate * optical)
    decay_sq = decay * decay
    denominator = eigen_rate + gamma_one + (eigen_rate - gamma_one) * decay_sq
    lost = (gamma_two * (1.0 - decay_sq) + 2.0 * eigen_rate * decay) / denominator
    return beam * (1.0 - lost)


def absorbed_mean(
    depth_wet, hot_extinction_thickness, above_wet, above_warm, absorption, continuum, albedo
):
    band_total = absorption.shape[0]
    band_group = min(8, band_total)
    unit_shape = (1,) * depth_wet.ndim
    running = jnp.zeros_like(depth_wet)
    for band_start in range(0, band_total, band_group):
        absorb_part = absorption[band_start : band_start + band_group].reshape(
            (band_group,) + unit_shape
        )
        continuum_part = continuum[band_start : band_start + band_group].reshape(
            (band_group,) + unit_shape
        )
        reflectivity_share = albedo[band_start : band_start + band_group].reshape(
            (band_group,) + unit_shape
        )
        terms = absorbed_per_band(
            depth_wet[None],
            hot_extinction_thickness[None],
            above_wet[None],
            above_warm[None],
            absorb_part,
            continuum_part,
            reflectivity_share,
        )
        running = running + jnp.sum(terms, axis=0)
    return running / band_total


def local(fields, sl_weights, sl_tile, daylit, absorption, continuum, albedo, wave_ids, legendre):
    meridian_number = lax.axis_size("lon")
    lat_count = lax.axis_size("lat")
    lev_count = lax.axis_size("lev")
    wave_devices = lat_count * meridian_number
    field_count, lev_local, lat_local, lon_local = fields.shape
    tile_width = sl_weights.shape[-1]
    tile_count = lon_local // tile_width
    row_blocks = sl_tile.shape[0]
    block_rows = lat_local // row_blocks
    padded = with_halo(fields, (("lon", 3),), tile_width)
    source_ids = jnp.arange(tile_count, dtype=jnp.int32)[None, :] + 1 + sl_tile
    onehot = (
        source_ids[:, :, None] == jnp.arange(tile_count + 2, dtype=jnp.int32)[None, None, :]
    ).astype(jnp.float32)
    blocks = (sl_weights[:, :, :, None, :] * onehot[:, :, None, :, None]).reshape(
        row_blocks, lon_local, (tile_count + 2) * tile_width
    )
    padded_rows = padded.reshape(field_count, lev_local, row_blocks, block_rows, -1)
    departure_estimate = jnp.einsum(
        "flbrk,bnk->bflrn", padded_rows, blocks, precision=highest
    )
    departure_estimate = departure_estimate.transpose(1, 2, 0, 3, 4).reshape(
        field_count, lev_local, lat_local, lon_local
    )
    moisture = departure_estimate[2]
    thermal_state = departure_estimate[0]
    stratum_factor = 4.0 / (lev_local * lev_count)
    depth_wet = stratum_factor * (0.2 + moisture * moisture)
    hot_extinction_thickness = stratum_factor * (0.2 + thermal_state * thermal_state)
    prefix = carried_in(
        jnp.stack([jnp.sum(depth_wet, axis=0), jnp.sum(hot_extinction_thickness, axis=0)]), "lev"
    )
    prefix_wet, prefix_warm = prefix[0], prefix[1]
    wet_levels = []
    warm_levels = []
    for level in range(lev_local):
        wet_levels.append(prefix_wet)
        warm_levels.append(prefix_warm)
        prefix_wet = prefix_wet + depth_wet[level]
        prefix_warm = prefix_warm + hot_extinction_thickness[level]
    above_wet = jnp.stack(wet_levels, axis=0)
    above_warm = jnp.stack(warm_levels, axis=0)
    absorbed = absorbed_mean(
        depth_wet, hot_extinction_thickness, above_wet, above_warm, absorption, continuum, albedo
    )
    absorbed = absorbed.reshape(lev_local, lat_local, tile_count, tile_width)
    heating = (absorbed * daylit.astype(jnp.float32)[None, :, :, None]).reshape(
        lev_local, lat_local, lon_local
    )
    chunk_rows = lev_local * lat_local // meridian_number
    halves = lat_local // chunk_rows

    def to_sectors(block):
        lines = block.reshape(block.shape[0], meridian_number, chunk_rows, lon_local)
        return lax.all_to_all(lines, "lon", split_axis=1, concat_axis=1, tiled=True)

    sectors_rest = to_sectors(departure_estimate[1:])
    sectors_heat = to_sectors(departure_estimate[:1] + heat_rate * heating[None])
    lon_total = lon_local * meridian_number
    wave_total = wave_ids.shape[0]
    inner = jnp.arange(lon_local, dtype=jnp.int32)
    phases = wave_ids[:, None] * inner[None, :] % lon_total
    angles = phases.astype(jnp.float32) * (2.0 * math.pi / lon_total)
    scale = 1.0 / math.sqrt(lon_total)
    dft_table = jnp.concatenate([jnp.cos(angles) * scale, jnp.sin(angles) * scale], axis=0)
    turns = wave_ids[None, :] * jnp.arange(meridian_number, dtype=jnp.int32)[:, None] % meridian_number
    turn_angles = turns.astype(jnp.float32) * (2.0 * math.pi / meridian_number)
    turn_cos = jnp.cos(turn_angles)[:, None, :]
    turn_sin = jnp.sin(turn_angles)[:, None, :]

    def transform(sectors):
        partial = jnp.einsum("fdqn,wn->fdqw", sectors, dft_table, precision=highest)
        cos_part = partial[..., :wave_total]
        sin_part = partial[..., wave_total:]
        real_part = jnp.sum(turn_cos * cos_part - turn_sin * sin_part, axis=1)
        imag_part = -jnp.sum(turn_sin * cos_part + turn_cos * sin_part, axis=1)
        return jnp.stack([real_part, imag_part], axis=1)

    fourier = jnp.concatenate([transform(sectors_heat), transform(sectors_rest)], axis=0)
    waves_local = wave_total // wave_devices
    outgoing_waves = (
        fourier.reshape(field_count, 2, chunk_rows, wave_devices, waves_local)
        .transpose(3, 1, 4, 0, 2)
        .reshape(wave_devices, 2 * waves_local, field_count * chunk_rows)
    )
    arrived = lax.all_to_all(
        outgoing_waves, ("lat", "lon"), split_axis=0, concat_axis=0, tiled=True
    )
    arrived = arrived.reshape(
        lat_count, lev_local, halves, 2, waves_local, field_count, chunk_rows
    )
    spectral_in = arrived.transpose(4, 3, 5, 1, 0, 2, 6).reshape(
        waves_local, 2, field_count, lev_local, lat_count * lat_local
    )
    spectra = jnp.einsum(
        "mcfls,mns->mcfln",
        lax.all_gather(spectral_in, "lev", axis=3, tiled=True),
        legendre,
        precision=highest,
    )
    degree_local = legendre.shape[1]
    degrees = lax.axis_index("lev") * degree_local + jnp.arange(degree_local, dtype=jnp.int32)
    own_waves = lax.dynamic_slice_in_dim(
        wave_ids, lax.axis_index(("lat", "lon")) * waves_local, waves_local
    )
    keep_mask = degrees[None, :] >= own_waves[:, None]
    return jnp.where(keep_mask[:, None, None, None, :], spectra, 0.0)


def solution(mesh):
    in_specs = (
        P(None, "lev", "lat", "lon"),
        P("lat", "lon", None, None),
        P("lat", "lon"),
        P("lat", "lon"),
        P(),
        P(),
        P(),
        P(),
        P(("lat", "lon"), "lev", None),
    )
    out_specs = P(("lat", "lon"), None, None, None, "lev")
    return jax.shard_map(local, mesh=mesh, in_specs=in_specs, out_specs=out_specs, check_vma=False)
```

```python
import math

import jax
import jax.numpy as jnp
from jax import lax
from jax.sharding import PartitionSpec as P

highest = lax.Precision.HIGHEST
heat_rate = 6.0
asymmetry = 0.6


def with_halo(block, sides, width):
    for axis, dim in sides:
        count = lax.axis_size(axis)
        forward = [(i, i + 1) for i in range(count - 1)]
        forward.append((count - 1, 0))
        backward = [(target, source) for source, target in forward]
        low = lax.ppermute(
            lax.slice_in_dim(block, block.shape[dim] - width, None, axis=dim), axis, forward
        )
        high = lax.ppermute(lax.slice_in_dim(block, 0, width, axis=dim), axis, backward)
        block = jnp.concatenate([low, block, high], axis=dim)
    return block


def carried_in(planes, axis):
    mine = lax.axis_index(axis)
    pieces = lax.all_gather(planes, axis)
    count = pieces.shape[0]
    below = (jnp.arange(count, dtype=jnp.int32) < mine).reshape((count,) + (1,) * planes.ndim)
    return jnp.sum(jnp.where(below, pieces, 0.0), axis=0)


def absorbed_per_band(
    depth_wet,
    hot_extinction_thickness,
    above_wet,
    above_warm,
    absorb_part,
    continuum_part,
    reflectivity_share,
):
    gamma_one = (7.0 - reflectivity_share * (4.0 + 3.0 * asymmetry)) / 4.0
    gamma_two = -(1.0 - reflectivity_share * (4.0 - 3.0 * asymmetry)) / 4.0
    eigen_rate = jnp.sqrt(gamma_one * gamma_one - gamma_two * gamma_two)
    optical = absorb_part * depth_wet + continuum_part * hot_extinction_thickness
    beam = jnp.exp(-(absorb_part * above_wet + continuum_part * above_warm))
    decay = jnp.exp(-eigen_rate * optical)
    decay_sq = decay * decay
    denominator = eigen_rate + gamma_one + (eigen_rate - gamma_one) * decay_sq
    lost = (gamma_two * (1.0 - decay_sq) + 2.0 * eigen_rate * decay) / denominator
    return beam * (1.0 - lost)


def absorbed_mean(
    depth_wet, hot_extinction_thickness, above_wet, above_warm, absorption, continuum, albedo
):
    band_total = absorption.shape[0]
    band_group = min(8, band_total)
    unit_shape = (1,) * depth_wet.ndim
    running = jnp.zeros_like(depth_wet)
    for band_start in range(0, band_total, band_group):
        absorb_part = absorption[band_start : band_start + band_group].reshape(
            (band_group,) + unit_shape
        )
        continuum_part = continuum[band_start : band_start + band_group].reshape(
            (band_group,) + unit_shape
        )
        reflectivity_share = albedo[band_start : band_start + band_group].reshape(
            (band_group,) + unit_shape
        )
        terms = absorbed_per_band(
            depth_wet[None],
            hot_extinction_thickness[None],
            above_wet[None],
            above_warm[None],
            absorb_part,
            continuum_part,
            reflectivity_share,
        )
        running = running + jnp.sum(terms, axis=0)
    return running / band_total


def local(fields, sl_weights, sl_tile, daylit, absorption, continuum, albedo, wave_ids, legendre):
    meridian_number = lax.axis_size("lon")
    lat_count = lax.axis_size("lat")
    lev_count = lax.axis_size("lev")
    wave_devices = lat_count * meridian_number
    field_count, lev_local, lat_local, lon_local = fields.shape
    tile_width = sl_weights.shape[-1]
    tile_count = lon_local // tile_width
    row_blocks = sl_tile.shape[0]
    block_rows = lat_local // row_blocks
    padded = with_halo(fields, (("lon", 3),), tile_width)
    source_ids = jnp.arange(tile_count, dtype=jnp.int32)[None, :] + 1 + sl_tile
    onehot = (
        source_ids[:, :, None] == jnp.arange(tile_count + 2, dtype=jnp.int32)[None, None, :]
    ).astype(jnp.float32)
    lane_mask = jnp.repeat(onehot, tile_width, axis=-1) > 0.5
    blocks = jnp.where(
        lane_mask[:, :, None, :], jnp.tile(sl_weights, (1, 1, 1, tile_count + 2)), 0.0
    ).reshape(row_blocks, lon_local, (tile_count + 2) * tile_width)
    padded_rows = padded.reshape(field_count, lev_local, row_blocks, block_rows, -1)
    departure_estimate = jnp.einsum(
        "flbrk,bnk->bflrn", padded_rows, blocks, precision=highest
    )
    departure_estimate = departure_estimate.transpose(1, 2, 0, 3, 4).reshape(
        field_count, lev_local, lat_local, lon_local
    )
    moisture = departure_estimate[2]
    thermal_state = departure_estimate[0]
    stratum_factor = 4.0 / (lev_local * lev_count)
    depth_wet = stratum_factor * (0.2 + moisture * moisture)
    hot_extinction_thickness = stratum_factor * (0.2 + thermal_state * thermal_state)
    prefix = carried_in(
        jnp.stack([jnp.sum(depth_wet, axis=0), jnp.sum(hot_extinction_thickness, axis=0)]), "lev"
    )
    prefix_wet, prefix_warm = prefix[0], prefix[1]
    wet_levels = []
    warm_levels = []
    for level in range(lev_local):
        wet_levels.append(prefix_wet)
        warm_levels.append(prefix_warm)
        prefix_wet = prefix_wet + depth_wet[level]
        prefix_warm = prefix_warm + hot_extinction_thickness[level]
    above_wet = jnp.stack(wet_levels, axis=0)
    above_warm = jnp.stack(warm_levels, axis=0)
    absorbed = absorbed_mean(
        depth_wet, hot_extinction_thickness, above_wet, above_warm, absorption, continuum, albedo
    )
    absorbed = absorbed.reshape(lev_local, lat_local, tile_count, tile_width)
    heating = (absorbed * daylit.astype(jnp.float32)[None, :, :, None]).reshape(
        lev_local, lat_local, lon_local
    )
    chunk_rows = lev_local * lat_local // meridian_number
    halves = lat_local // chunk_rows

    def to_sectors(block):
        lines = block.reshape(block.shape[0], meridian_number, chunk_rows, lon_local)
        return lax.all_to_all(lines, "lon", split_axis=1, concat_axis=1, tiled=True)

    sectors_rest = to_sectors(departure_estimate[1:])
    sectors_heat = to_sectors(departure_estimate[:1] + heat_rate * heating[None])
    lon_total = lon_local * meridian_number
    wave_total = wave_ids.shape[0]
    inner = jnp.arange(lon_local, dtype=jnp.int32)
    phases = wave_ids[:, None] * inner[None, :] % lon_total
    angles = phases.astype(jnp.float32) * (2.0 * math.pi / lon_total)
    scale = 1.0 / math.sqrt(lon_total)
    dft_table = jnp.concatenate([jnp.cos(angles) * scale, jnp.sin(angles) * scale], axis=0)
    turns = wave_ids[None, :] * jnp.arange(meridian_number, dtype=jnp.int32)[:, None] % meridian_number
    turn_angles = turns.astype(jnp.float32) * (2.0 * math.pi / meridian_number)
    turn_cos = jnp.cos(turn_angles)[:, None, :]
    turn_sin = jnp.sin(turn_angles)[:, None, :]

    def transform(sectors):
        partial = jnp.einsum("fdqn,wn->fdqw", sectors, dft_table, precision=highest)
        cos_part = partial[..., :wave_total]
        sin_part = partial[..., wave_total:]
        real_part = jnp.sum(turn_cos * cos_part - turn_sin * sin_part, axis=1)
        imag_part = -jnp.sum(turn_sin * cos_part + turn_cos * sin_part, axis=1)
        return jnp.stack([real_part, imag_part], axis=1)

    fourier = jnp.concatenate([transform(sectors_heat), transform(sectors_rest)], axis=0)
    waves_local = wave_total // wave_devices
    outgoing_waves = (
        fourier.reshape(field_count, 2, chunk_rows, wave_devices, waves_local)
        .transpose(3, 1, 4, 0, 2)
        .reshape(wave_devices, 2 * waves_local, field_count * chunk_rows)
    )
    arrived = lax.all_to_all(
        outgoing_waves, ("lat", "lon"), split_axis=0, concat_axis=0, tiled=True
    )
    arrived = arrived.reshape(
        lat_count, lev_local, halves, 2, waves_local, field_count, chunk_rows
    )
    spectral_in = arrived.transpose(4, 3, 5, 1, 0, 2, 6).reshape(
        waves_local, 2 * field_count * lev_local, lat_count * lat_local
    )
    gathered = lax.all_gather(spectral_in, "lev", axis=0).transpose(1, 0, 2, 3)
    spectra = jnp.einsum("skqp,snp->skqn", gathered, legendre, precision=highest)
    spectra = (
        spectra.reshape(waves_local, lev_count, 2, field_count, lev_local, -1)
        .transpose(0, 2, 3, 1, 4, 5)
        .reshape(waves_local, 2, field_count, lev_count * lev_local, -1)
    )
    degree_local = legendre.shape[1]
    degrees = lax.axis_index("lev") * degree_local + jnp.arange(degree_local, dtype=jnp.int32)
    own_waves = lax.dynamic_slice_in_dim(
        wave_ids, lax.axis_index(("lat", "lon")) * waves_local, waves_local
    )
    keep_mask = degrees[None, :] >= own_waves[:, None]
    return jnp.where(keep_mask[:, None, None, None, :], spectra, 0.0)


def solution(mesh):
    in_specs = (
        P(None, "lev", "lat", "lon"),
        P("lat", "lon", None, None),
        P("lat", "lon"),
        P("lat", "lon"),
        P(),
        P(),
        P(),
        P(),
        P(("lat", "lon"), "lev", None),
    )
    out_specs = P(("lat", "lon"), None, None, None, "lev")
    return jax.shard_map(local, mesh=mesh, in_specs=in_specs, out_specs=out_specs, check_vma=False)
```

```python
import math

import jax
import jax.numpy as jnp
from jax import lax
from jax.sharding import PartitionSpec as P

highest = lax.Precision.HIGHEST
heat_rate = 6.0
asymmetry = 0.6


def with_halo(block, sides, width):
    for axis, dim in sides:
        count = lax.axis_size(axis)
        forward = [(i, i + 1) for i in range(count - 1)]
        forward.append((count - 1, 0))
        backward = [(target, source) for source, target in forward]
        low = lax.ppermute(
            lax.slice_in_dim(block, block.shape[dim] - width, None, axis=dim), axis, forward
        )
        high = lax.ppermute(lax.slice_in_dim(block, 0, width, axis=dim), axis, backward)
        block = jnp.concatenate([low, block, high], axis=dim)
    return block


def carried_in(planes, axis):
    mine = lax.axis_index(axis)
    pieces = lax.all_gather(planes, axis)
    count = pieces.shape[0]
    below = (jnp.arange(count, dtype=jnp.int32) < mine).reshape((count,) + (1,) * planes.ndim)
    return jnp.sum(jnp.where(below, pieces, 0.0), axis=0)


def absorbed_per_band(
    depth_wet,
    hot_extinction_thickness,
    above_wet,
    above_warm,
    absorb_part,
    continuum_part,
    reflectivity_share,
):
    gamma_one = (7.0 - reflectivity_share * (4.0 + 3.0 * asymmetry)) / 4.0
    gamma_two = -(1.0 - reflectivity_share * (4.0 - 3.0 * asymmetry)) / 4.0
    eigen_rate = jnp.sqrt(gamma_one * gamma_one - gamma_two * gamma_two)
    optical = absorb_part * depth_wet + continuum_part * hot_extinction_thickness
    beam = jnp.exp(-(absorb_part * above_wet + continuum_part * above_warm))
    decay = jnp.exp(-eigen_rate * optical)
    decay_sq = decay * decay
    denominator = eigen_rate + gamma_one + (eigen_rate - gamma_one) * decay_sq
    lost = (gamma_two * (1.0 - decay_sq) + 2.0 * eigen_rate * decay) / denominator
    return beam * (1.0 - lost)


def absorbed_mean(
    depth_wet, hot_extinction_thickness, above_wet, above_warm, absorption, continuum, albedo
):
    band_total = absorption.shape[0]
    band_group = min(8, band_total)
    unit_shape = (1,) * depth_wet.ndim
    running = jnp.zeros_like(depth_wet)
    for band_start in range(0, band_total, band_group):
        absorb_part = absorption[band_start : band_start + band_group].reshape(
            (band_group,) + unit_shape
        )
        continuum_part = continuum[band_start : band_start + band_group].reshape(
            (band_group,) + unit_shape
        )
        reflectivity_share = albedo[band_start : band_start + band_group].reshape(
            (band_group,) + unit_shape
        )
        terms = absorbed_per_band(
            depth_wet[None],
            hot_extinction_thickness[None],
            above_wet[None],
            above_warm[None],
            absorb_part,
            continuum_part,
            reflectivity_share,
        )
        running = running + jnp.sum(terms, axis=0)
    return running / band_total


def local(fields, sl_weights, sl_tile, daylit, absorption, continuum, albedo, wave_ids, legendre):
    meridian_number = lax.axis_size("lon")
    lat_count = lax.axis_size("lat")
    lev_count = lax.axis_size("lev")
    wave_devices = lat_count * meridian_number
    field_count, lev_local, lat_local, lon_local = fields.shape
    tile_width = sl_weights.shape[-1]
    tile_count = lon_local // tile_width
    row_blocks = sl_tile.shape[0]
    block_rows = lat_local // row_blocks
    padded = with_halo(fields, (("lon", 3),), tile_width)
    source_ids = jnp.arange(tile_count, dtype=jnp.int32)[None, :] + 1 + sl_tile
    onehot = (
        source_ids[:, :, None] == jnp.arange(tile_count + 2, dtype=jnp.int32)[None, None, :]
    ).astype(jnp.float32)
    lane_mask = jnp.repeat(onehot, tile_width, axis=-1) > 0.5
    blocks = jnp.where(
        lane_mask[:, :, None, :], jnp.tile(sl_weights, (1, 1, 1, tile_count + 2)), 0.0
    ).reshape(row_blocks, lon_local, (tile_count + 2) * tile_width)
    padded_rows = padded.reshape(field_count, lev_local, row_blocks, block_rows, -1)
    departure_estimate = jnp.einsum(
        "flbrk,bnk->bflrn", padded_rows, blocks, precision=highest
    )
    departure_estimate = departure_estimate.transpose(1, 2, 0, 3, 4).reshape(
        field_count, lev_local, lat_local, lon_local
    )
    moisture = departure_estimate[2]
    thermal_state = departure_estimate[0]
    stratum_factor = 4.0 / (lev_local * lev_count)
    depth_wet = stratum_factor * (0.2 + moisture * moisture)
    hot_extinction_thickness = stratum_factor * (0.2 + thermal_state * thermal_state)
    prefix = carried_in(
        jnp.stack([jnp.sum(depth_wet, axis=0), jnp.sum(hot_extinction_thickness, axis=0)]), "lev"
    )
    prefix_wet, prefix_warm = prefix[0], prefix[1]
    wet_levels = []
    warm_levels = []
    for level in range(lev_local):
        wet_levels.append(prefix_wet)
        warm_levels.append(prefix_warm)
        prefix_wet = prefix_wet + depth_wet[level]
        prefix_warm = prefix_warm + hot_extinction_thickness[level]
    above_wet = jnp.stack(wet_levels, axis=0)
    above_warm = jnp.stack(warm_levels, axis=0)
    absorbed = absorbed_mean(
        depth_wet, hot_extinction_thickness, above_wet, above_warm, absorption, continuum, albedo
    )
    absorbed = absorbed.reshape(lev_local, lat_local, tile_count, tile_width)
    heating = (absorbed * daylit.astype(jnp.float32)[None, :, :, None]).reshape(
        lev_local, lat_local, lon_local
    )
    chunk_rows = lev_local * lat_local // meridian_number
    halves = lat_local // chunk_rows

    def to_sectors(block):
        lines = block.reshape(block.shape[0], meridian_number, chunk_rows, lon_local)
        return lax.all_to_all(lines, "lon", split_axis=1, concat_axis=1, tiled=True)

    sectors_rest = to_sectors(departure_estimate[1:])
    sectors_heat = to_sectors(departure_estimate[:1] + heat_rate * heating[None])
    lon_total = lon_local * meridian_number
    wave_total = wave_ids.shape[0]
    inner = jnp.arange(lon_local, dtype=jnp.int32)
    phases = wave_ids[:, None] * inner[None, :] % lon_total
    angles = phases.astype(jnp.float32) * (2.0 * math.pi / lon_total)
    scale = 1.0 / math.sqrt(lon_total)
    dft_table = jnp.concatenate([jnp.cos(angles) * scale, jnp.sin(angles) * scale], axis=0)
    turns = wave_ids[None, :] * jnp.arange(meridian_number, dtype=jnp.int32)[:, None] % meridian_number
    turn_angles = turns.astype(jnp.float32) * (2.0 * math.pi / meridian_number)
    turn_cos = jnp.cos(turn_angles)[:, None, :]
    turn_sin = jnp.sin(turn_angles)[:, None, :]

    def transform(sectors):
        partial = jnp.einsum("fdqn,wn->fdqw", sectors, dft_table, precision=highest)
        cos_part = partial[..., :wave_total]
        sin_part = partial[..., wave_total:]
        real_part = jnp.sum(turn_cos * cos_part - turn_sin * sin_part, axis=1)
        imag_part = -jnp.sum(turn_sin * cos_part + turn_cos * sin_part, axis=1)
        return jnp.stack([real_part, imag_part], axis=1)

    fourier = jnp.concatenate([transform(sectors_heat), transform(sectors_rest)], axis=0)
    waves_local = wave_total // wave_devices
    outgoing_waves = (
        fourier.reshape(field_count, 2, chunk_rows, wave_devices, waves_local)
        .transpose(3, 1, 4, 0, 2)
        .reshape(wave_devices, 2 * waves_local, field_count * chunk_rows)
    )
    arrived = lax.all_to_all(
        outgoing_waves, ("lat", "lon"), split_axis=0, concat_axis=0, tiled=True
    )
    arrived = arrived.reshape(
        lat_count, lev_local, halves, 2, waves_local, field_count, chunk_rows
    )
    spectral_in = arrived.transpose(4, 3, 5, 1, 0, 2, 6).reshape(
        waves_local, 2 * field_count * lev_local, lat_count * lat_local
    )
    lev_here = lax.axis_index("lev")
    pieces = [spectral_in]
    for shift in range(1, lev_count):
        pieces.append(
            lax.ppermute(
                spectral_in, "lev", [(k, (k + shift) % lev_count) for k in range(lev_count)]
            )
        )
    by_offset = jnp.stack([pieces[(-t) % lev_count] for t in range(lev_count)] * 2, axis=1)
    gathered = lax.dynamic_slice_in_dim(by_offset, lev_count - lev_here, lev_count, axis=1)
    spectra = jnp.einsum("skqp,snp->skqn", gathered, legendre, precision=highest)
    spectra = (
        spectra.reshape(waves_local, lev_count, 2, field_count, lev_local, -1)
        .transpose(0, 2, 3, 1, 4, 5)
        .reshape(waves_local, 2, field_count, lev_count * lev_local, -1)
    )
    degree_local = legendre.shape[1]
    degrees = lax.axis_index("lev") * degree_local + jnp.arange(degree_local, dtype=jnp.int32)
    own_waves = lax.dynamic_slice_in_dim(
        wave_ids, lax.axis_index(("lat", "lon")) * waves_local, waves_local
    )
    keep_mask = degrees[None, :] >= own_waves[:, None]
    return jnp.where(keep_mask[:, None, None, None, :], spectra, 0.0)


def solution(mesh):
    in_specs = (
        P(None, "lev", "lat", "lon"),
        P("lat", "lon", None, None),
        P("lat", "lon"),
        P("lat", "lon"),
        P(),
        P(),
        P(),
        P(),
        P(("lat", "lon"), "lev", None),
    )
    out_specs = P(("lat", "lon"), None, None, None, "lev")
    return jax.shard_map(local, mesh=mesh, in_specs=in_specs, out_specs=out_specs, check_vma=False)
```

```python
import math

import jax
import jax.numpy as jnp
from jax import lax
from jax.sharding import PartitionSpec as P

highest = lax.Precision.HIGHEST
heat_rate = 6.0
asymmetry = 0.6


def with_halo(block, sides, width):
    for axis, dim in sides:
        count = lax.axis_size(axis)
        forward = [(i, i + 1) for i in range(count - 1)]
        forward.append((count - 1, 0))
        backward = [(target, source) for source, target in forward]
        low = lax.ppermute(
            lax.slice_in_dim(block, block.shape[dim] - width, None, axis=dim), axis, forward
        )
        high = lax.ppermute(lax.slice_in_dim(block, 0, width, axis=dim), axis, backward)
        block = jnp.concatenate([low, block, high], axis=dim)
    return block


def carried_in(planes, axis):
    mine = lax.axis_index(axis)
    pieces = lax.all_gather(planes, axis)
    count = pieces.shape[0]
    below = (jnp.arange(count, dtype=jnp.int32) < mine).reshape((count,) + (1,) * planes.ndim)
    return jnp.sum(jnp.where(below, pieces, 0.0), axis=0)


def absorbed_per_band(
    depth_wet,
    hot_extinction_thickness,
    above_wet,
    above_warm,
    absorb_part,
    continuum_part,
    reflectivity_share,
):
    gamma_one = (7.0 - reflectivity_share * (4.0 + 3.0 * asymmetry)) / 4.0
    gamma_two = -(1.0 - reflectivity_share * (4.0 - 3.0 * asymmetry)) / 4.0
    eigen_rate = jnp.sqrt(gamma_one * gamma_one - gamma_two * gamma_two)
    optical = absorb_part * depth_wet + continuum_part * hot_extinction_thickness
    beam = jnp.exp(-(absorb_part * above_wet + continuum_part * above_warm))
    decay = jnp.exp(-eigen_rate * optical)
    decay_sq = decay * decay
    denominator = eigen_rate + gamma_one + (eigen_rate - gamma_one) * decay_sq
    lost = (gamma_two * (1.0 - decay_sq) + 2.0 * eigen_rate * decay) / denominator
    return beam * (1.0 - lost)


def absorbed_mean(
    depth_wet, hot_extinction_thickness, above_wet, above_warm, absorption, continuum, albedo
):
    band_total = absorption.shape[0]
    band_group = min(8, band_total)
    unit_shape = (1,) * depth_wet.ndim
    running = jnp.zeros_like(depth_wet)
    for band_start in range(0, band_total, band_group):
        absorb_part = absorption[band_start : band_start + band_group].reshape(
            (band_group,) + unit_shape
        )
        continuum_part = continuum[band_start : band_start + band_group].reshape(
            (band_group,) + unit_shape
        )
        reflectivity_share = albedo[band_start : band_start + band_group].reshape(
            (band_group,) + unit_shape
        )
        terms = absorbed_per_band(
            depth_wet[None],
            hot_extinction_thickness[None],
            above_wet[None],
            above_warm[None],
            absorb_part,
            continuum_part,
            reflectivity_share,
        )
        running = running + jnp.sum(terms, axis=0)
    return running / band_total


def local(fields, sl_weights, sl_tile, daylit, absorption, continuum, albedo, wave_ids, legendre):
    meridian_number = lax.axis_size("lon")
    lat_count = lax.axis_size("lat")
    lev_count = lax.axis_size("lev")
    wave_devices = lat_count * meridian_number
    field_count, lev_local, lat_local, lon_local = fields.shape
    tile_width = sl_weights.shape[-1]
    tile_count = lon_local // tile_width
    row_blocks = sl_tile.shape[0]
    block_rows = lat_local // row_blocks
    padded = with_halo(fields, (("lon", 3),), tile_width)
    source_ids = jnp.arange(tile_count, dtype=jnp.int32)[None, :] + 1 + sl_tile
    onehot = (
        source_ids[:, :, None] == jnp.arange(tile_count + 2, dtype=jnp.int32)[None, None, :]
    ).astype(jnp.float32)
    lane_mask = jnp.repeat(onehot, tile_width, axis=-1) > 0.5
    blocks = jnp.where(
        lane_mask[:, :, None, :], jnp.tile(sl_weights, (1, 1, 1, tile_count + 2)), 0.0
    ).reshape(row_blocks, lon_local, (tile_count + 2) * tile_width)
    padded_rows = padded.reshape(field_count, lev_local, row_blocks, block_rows, -1)
    departure_estimate = jnp.einsum(
        "flbrk,bnk->bflrn", padded_rows, blocks, precision=highest
    )
    departure_estimate = departure_estimate.transpose(1, 2, 0, 3, 4).reshape(
        field_count, lev_local, lat_local, lon_local
    )
    moisture = departure_estimate[2]
    thermal_state = departure_estimate[0]
    stratum_factor = 4.0 / (lev_local * lev_count)
    depth_wet = stratum_factor * (0.2 + moisture * moisture)
    hot_extinction_thickness = stratum_factor * (0.2 + thermal_state * thermal_state)
    prefix = carried_in(
        jnp.stack([jnp.sum(depth_wet, axis=0), jnp.sum(hot_extinction_thickness, axis=0)]), "lev"
    )
    prefix_wet, prefix_warm = prefix[0], prefix[1]
    wet_levels = []
    warm_levels = []
    for level in range(lev_local):
        wet_levels.append(prefix_wet)
        warm_levels.append(prefix_warm)
        prefix_wet = prefix_wet + depth_wet[level]
        prefix_warm = prefix_warm + hot_extinction_thickness[level]
    above_wet = jnp.stack(wet_levels, axis=0)
    above_warm = jnp.stack(warm_levels, axis=0)
    absorbed = absorbed_mean(
        depth_wet, hot_extinction_thickness, above_wet, above_warm, absorption, continuum, albedo
    )
    absorbed = absorbed.reshape(lev_local, lat_local, tile_count, tile_width)
    heating = (absorbed * daylit.astype(jnp.float32)[None, :, :, None]).reshape(
        lev_local, lat_local, lon_local
    )
    chunk_rows = lev_local * lat_local // meridian_number
    halves = lat_local // chunk_rows

    def to_sectors(block):
        lines = block.reshape(block.shape[0], meridian_number, chunk_rows, lon_local)
        return lax.all_to_all(lines, "lon", split_axis=1, concat_axis=1, tiled=True)

    sectors_rest = to_sectors(departure_estimate[1:])
    sectors_heat = to_sectors(departure_estimate[:1] + heat_rate * heating[None])
    lon_total = lon_local * meridian_number
    wave_total = wave_ids.shape[0]
    inner = jnp.arange(lon_local, dtype=jnp.int32)
    phases = wave_ids[:, None] * inner[None, :] % lon_total
    angles = phases.astype(jnp.float32) * (2.0 * math.pi / lon_total)
    scale = 1.0 / math.sqrt(lon_total)
    dft_table = jnp.concatenate([jnp.cos(angles) * scale, jnp.sin(angles) * scale], axis=0)
    turns = wave_ids[None, :] * jnp.arange(meridian_number, dtype=jnp.int32)[:, None] % meridian_number
    turn_angles = turns.astype(jnp.float32) * (2.0 * math.pi / meridian_number)
    turn_cos = jnp.cos(turn_angles)[:, None, :]
    turn_sin = jnp.sin(turn_angles)[:, None, :]

    def transform(sectors):
        partial = jnp.einsum("fdqn,wn->fdqw", sectors, dft_table, precision=highest)
        cos_part = partial[..., :wave_total]
        sin_part = partial[..., wave_total:]
        real_part = jnp.sum(turn_cos * cos_part - turn_sin * sin_part, axis=1)
        imag_part = -jnp.sum(turn_sin * cos_part + turn_cos * sin_part, axis=1)
        return jnp.stack([real_part, imag_part], axis=1)

    fourier = jnp.concatenate([transform(sectors_heat), transform(sectors_rest)], axis=0)
    waves_local = wave_total // wave_devices
    outgoing_waves = (
        fourier.reshape(field_count, 2, chunk_rows, wave_devices, waves_local)
        .transpose(3, 1, 4, 0, 2)
        .reshape(wave_devices, 2 * waves_local, field_count * chunk_rows)
    )
    arrived = lax.all_to_all(
        outgoing_waves, ("lat", "lon"), split_axis=0, concat_axis=0, tiled=True
    )
    arrived = arrived.reshape(
        lat_count, lev_local, halves, 2, waves_local, field_count, chunk_rows
    )
    spectral_in = arrived.transpose(4, 3, 5, 1, 0, 2, 6).reshape(
        waves_local, 2 * field_count * lev_local, lat_count * lat_local
    )
    lev_here = lax.axis_index("lev")

    def swap(value, flip):
        return lax.ppermute(value, "lev", [(k, k ^ flip) for k in range(lev_count)])

    across = swap(spectral_in, 2)
    by_flip = jnp.stack(
        [spectral_in, swap(spectral_in, 1), across, swap(across, 1)], axis=1
    )
    flipped = jnp.einsum("skqp,snp->skqn", by_flip, legendre, precision=highest)
    flipped = jnp.where((lev_here & 1) == 1, flipped[:, jnp.array([1, 0, 3, 2])], flipped)
    spectra = jnp.where((lev_here & 2) == 2, flipped[:, jnp.array([2, 3, 0, 1])], flipped)
    spectra = (
        spectra.reshape(waves_local, lev_count, 2, field_count, lev_local, -1)
        .transpose(0, 2, 3, 1, 4, 5)
        .reshape(waves_local, 2, field_count, lev_count * lev_local, -1)
    )
    degree_local = legendre.shape[1]
    degrees = lax.axis_index("lev") * degree_local + jnp.arange(degree_local, dtype=jnp.int32)
    own_waves = lax.dynamic_slice_in_dim(
        wave_ids, lax.axis_index(("lat", "lon")) * waves_local, waves_local
    )
    keep_mask = degrees[None, :] >= own_waves[:, None]
    return jnp.where(keep_mask[:, None, None, None, :], spectra, 0.0)


def solution(mesh):
    in_specs = (
        P(None, "lev", "lat", "lon"),
        P("lat", "lon", None, None),
        P("lat", "lon"),
        P("lat", "lon"),
        P(),
        P(),
        P(),
        P(),
        P(("lat", "lon"), "lev", None),
    )
    out_specs = P(("lat", "lon"), None, None, None, "lev")
    return jax.shard_map(local, mesh=mesh, in_specs=in_specs, out_specs=out_specs, check_vma=False)
```

```python
import math

import jax
import jax.numpy as jnp
from jax import lax
from jax.sharding import PartitionSpec as P

highest = lax.Precision.HIGHEST
heat_rate = 6.0
asymmetry = 0.6


def with_halo(block, sides, width):
    for axis, dim in sides:
        count = lax.axis_size(axis)
        forward = [(i, i + 1) for i in range(count - 1)]
        forward.append((count - 1, 0))
        backward = [(target, source) for source, target in forward]
        low = lax.ppermute(
            lax.slice_in_dim(block, block.shape[dim] - width, None, axis=dim), axis, forward
        )
        high = lax.ppermute(lax.slice_in_dim(block, 0, width, axis=dim), axis, backward)
        block = jnp.concatenate([low, block, high], axis=dim)
    return block


def carried_in(planes, axis):
    count, mine = (lax.axis_size(axis), lax.axis_index(axis))
    if count != 4:
        pieces = lax.all_gather(planes, axis)
        below = (jnp.arange(count, dtype=jnp.int32) < mine).reshape((count,) + (1,) * planes.ndim)
        return jnp.sum(jnp.where(below, pieces, 0.0), axis=0)
    partner = lax.ppermute(planes, axis, [(k, k ^ 1) for k in range(count)])
    lower = lax.ppermute(planes + partner, axis, [(0, 2), (1, 3)])
    return lower + jnp.where(mine % 2 == 1, partner, 0.0)


def absorbed_per_band(
    depth_wet,
    hot_extinction_thickness,
    above_wet,
    above_warm,
    absorb_part,
    continuum_part,
    reflectivity_share,
):
    gamma_one = (7.0 - reflectivity_share * (4.0 + 3.0 * asymmetry)) / 4.0
    gamma_two = -(1.0 - reflectivity_share * (4.0 - 3.0 * asymmetry)) / 4.0
    eigen_rate = jnp.sqrt(gamma_one * gamma_one - gamma_two * gamma_two)
    optical = absorb_part * depth_wet + continuum_part * hot_extinction_thickness
    beam = jnp.exp(-(absorb_part * above_wet + continuum_part * above_warm))
    decay = jnp.exp(-eigen_rate * optical)
    decay_sq = decay * decay
    denominator = eigen_rate + gamma_one + (eigen_rate - gamma_one) * decay_sq
    lost = (gamma_two * (1.0 - decay_sq) + 2.0 * eigen_rate * decay) / denominator
    return beam * (1.0 - lost)


def absorbed_mean(
    depth_wet, hot_extinction_thickness, above_wet, above_warm, absorption, continuum, albedo
):
    band_total = absorption.shape[0]
    band_group = min(8, band_total)
    unit_shape = (1,) * depth_wet.ndim
    running = jnp.zeros_like(depth_wet)
    for band_start in range(0, band_total, band_group):
        absorb_part = absorption[band_start : band_start + band_group].reshape(
            (band_group,) + unit_shape
        )
        continuum_part = continuum[band_start : band_start + band_group].reshape(
            (band_group,) + unit_shape
        )
        reflectivity_share = albedo[band_start : band_start + band_group].reshape(
            (band_group,) + unit_shape
        )
        terms = absorbed_per_band(
            depth_wet[None],
            hot_extinction_thickness[None],
            above_wet[None],
            above_warm[None],
            absorb_part,
            continuum_part,
            reflectivity_share,
        )
        running = running + jnp.sum(terms, axis=0)
    return running / band_total


def local(fields, sl_weights, sl_tile, daylit, absorption, continuum, albedo, wave_ids, legendre):
    meridian_number = lax.axis_size("lon")
    lat_count = lax.axis_size("lat")
    lev_count = lax.axis_size("lev")
    wave_devices = lat_count * meridian_number
    field_count, lev_local, lat_local, lon_local = fields.shape
    tile_width = sl_weights.shape[-1]
    tile_count = lon_local // tile_width
    row_blocks = sl_tile.shape[0]
    block_rows = lat_local // row_blocks
    count = lax.axis_size("lon")
    forward = [(i, (i + 1) % count) for i in range(count)]
    backward = [(target, source) for source, target in forward]
    left = lax.ppermute(fields[..., lon_local - tile_width :], "lon", forward)
    right = lax.ppermute(fields[..., :tile_width], "lon", backward)
    tiles = [left] + [
        fields[..., j * tile_width : (j + 1) * tile_width] for j in range(tile_count)
    ] + [right]
    tile_shape = (field_count, lev_local, row_blocks, block_rows, tile_width)
    outputs = []
    for j in range(tile_count):
        offset = sl_tile[:, j].reshape(1, 1, row_blocks, 1, 1)
        source = jnp.where(
            offset < 0,
            tiles[j].reshape(tile_shape),
            jnp.where(offset > 0, tiles[j + 2].reshape(tile_shape), tiles[j + 1].reshape(tile_shape)),
        )
        outputs.append(
            jnp.einsum("flbrc,btc->bflrt", source, sl_weights[:, j], precision=highest)
        )
    departure_estimate = jnp.concatenate(outputs, axis=-1).transpose(1, 2, 0, 3, 4).reshape(
        field_count, lev_local, lat_local, lon_local
    )
    moisture = departure_estimate[2]
    thermal_state = departure_estimate[0]
    stratum_factor = 4.0 / (lev_local * lev_count)
    depth_wet = stratum_factor * (0.2 + moisture * moisture)
    hot_extinction_thickness = stratum_factor * (0.2 + thermal_state * thermal_state)
    prefix = carried_in(
        jnp.stack([jnp.sum(depth_wet, axis=0), jnp.sum(hot_extinction_thickness, axis=0)]), "lev"
    )
    prefix_wet, prefix_warm = prefix[0], prefix[1]
    wet_levels = []
    warm_levels = []
    for level in range(lev_local):
        wet_levels.append(prefix_wet)
        warm_levels.append(prefix_warm)
        prefix_wet = prefix_wet + depth_wet[level]
        prefix_warm = prefix_warm + hot_extinction_thickness[level]
    above_wet = jnp.stack(wet_levels, axis=0)
    above_warm = jnp.stack(warm_levels, axis=0)
    absorbed = absorbed_mean(
        depth_wet, hot_extinction_thickness, above_wet, above_warm, absorption, continuum, albedo
    )
    absorbed = absorbed.reshape(lev_local, lat_local, tile_count, tile_width)
    heating = (absorbed * daylit.astype(jnp.float32)[None, :, :, None]).reshape(
        lev_local, lat_local, lon_local
    )
    chunk_rows = lev_local * lat_local // meridian_number
    halves = lat_local // chunk_rows

    def to_sectors(block):
        lines = block.reshape(block.shape[0], meridian_number, chunk_rows, lon_local)
        return lax.all_to_all(lines, "lon", split_axis=1, concat_axis=1, tiled=True)

    sectors_rest = to_sectors(departure_estimate[1:])
    sectors_heat = to_sectors(departure_estimate[:1] + heat_rate * heating[None])
    lon_total = lon_local * meridian_number
    wave_total = wave_ids.shape[0]
    inner = jnp.arange(lon_local, dtype=jnp.int32)
    phases = wave_ids[:, None] * inner[None, :] % lon_total
    angles = phases.astype(jnp.float32) * (2.0 * math.pi / lon_total)
    scale = 1.0 / math.sqrt(lon_total)
    dft_table = jnp.concatenate([jnp.cos(angles) * scale, jnp.sin(angles) * scale], axis=0)
    turns = wave_ids[None, :] * jnp.arange(meridian_number, dtype=jnp.int32)[:, None] % meridian_number
    turn_angles = turns.astype(jnp.float32) * (2.0 * math.pi / meridian_number)
    turn_cos = jnp.cos(turn_angles)[:, None, :]
    turn_sin = jnp.sin(turn_angles)[:, None, :]

    def transform(sectors):
        partial = jnp.einsum("fdqn,wn->fdqw", sectors, dft_table, precision=highest)
        cos_part = partial[..., :wave_total]
        sin_part = partial[..., wave_total:]
        real_part = jnp.sum(turn_cos * cos_part - turn_sin * sin_part, axis=1)
        imag_part = -jnp.sum(turn_sin * cos_part + turn_cos * sin_part, axis=1)
        return jnp.stack([real_part, imag_part], axis=1)

    fourier = jnp.concatenate([transform(sectors_heat), transform(sectors_rest)], axis=0)
    waves_local = wave_total // wave_devices
    outgoing_waves = (
        fourier.reshape(field_count, 2, chunk_rows, wave_devices, waves_local)
        .transpose(3, 1, 4, 0, 2)
        .reshape(wave_devices, 2 * waves_local, field_count * chunk_rows)
    )
    arrived = lax.all_to_all(
        outgoing_waves, ("lat", "lon"), split_axis=0, concat_axis=0, tiled=True
    )
    arrived = arrived.reshape(
        lat_count, lev_local, halves, 2, waves_local, field_count, chunk_rows
    )
    spectral_in = arrived.transpose(4, 3, 5, 1, 0, 2, 6).reshape(
        waves_local, 2 * field_count * lev_local, lat_count * lat_local
    )
    lev_here = lax.axis_index("lev")

    def swap(value, flip):
        return lax.ppermute(value, "lev", [(k, k ^ flip) for k in range(lev_count)])

    across = swap(spectral_in, 2)
    by_flip = jnp.stack(
        [spectral_in, swap(spectral_in, 1), across, swap(across, 1)], axis=1
    )
    flipped = jnp.einsum("skqp,snp->skqn", by_flip, legendre, precision=highest)
    flipped = jnp.where((lev_here & 1) == 1, flipped[:, jnp.array([1, 0, 3, 2])], flipped)
    spectra = jnp.where((lev_here & 2) == 2, flipped[:, jnp.array([2, 3, 0, 1])], flipped)
    spectra = (
        spectra.reshape(waves_local, lev_count, 2, field_count, lev_local, -1)
        .transpose(0, 2, 3, 1, 4, 5)
        .reshape(waves_local, 2, field_count, lev_count * lev_local, -1)
    )
    degree_local = legendre.shape[1]
    degrees = lax.axis_index("lev") * degree_local + jnp.arange(degree_local, dtype=jnp.int32)
    own_waves = lax.dynamic_slice_in_dim(
        wave_ids, lax.axis_index(("lat", "lon")) * waves_local, waves_local
    )
    keep_mask = degrees[None, :] >= own_waves[:, None]
    return jnp.where(keep_mask[:, None, None, None, :], spectra, 0.0)


def solution(mesh):
    in_specs = (
        P(None, "lev", "lat", "lon"),
        P("lat", "lon", None, None),
        P("lat", "lon"),
        P("lat", "lon"),
        P(),
        P(),
        P(),
        P(),
        P(("lat", "lon"), "lev", None),
    )
    out_specs = P(("lat", "lon"), None, None, None, "lev")
    return jax.shard_map(local, mesh=mesh, in_specs=in_specs, out_specs=out_specs, check_vma=False)
```

```python
import math

import jax
import jax.numpy as jnp
from jax import lax
from jax.sharding import PartitionSpec as P

highest = lax.Precision.HIGHEST
heat_rate = 6.0
asymmetry = 0.6


def carried_in(planes, axis):
    mine = lax.axis_index(axis)
    pieces = lax.all_gather(planes, axis)
    count = pieces.shape[0]
    below = (jnp.arange(count, dtype=jnp.int32) < mine).reshape((count,) + (1,) * planes.ndim)
    return jnp.sum(jnp.where(below, pieces, 0.0), axis=0)


def absorbed_per_band(
    depth_wet,
    hot_extinction_thickness,
    above_wet,
    above_warm,
    absorb_part,
    continuum_part,
    reflectivity_share,
):
    gamma_one = (7.0 - reflectivity_share * (4.0 + 3.0 * asymmetry)) / 4.0
    gamma_two = -(1.0 - reflectivity_share * (4.0 - 3.0 * asymmetry)) / 4.0
    eigen_rate = jnp.sqrt(gamma_one * gamma_one - gamma_two * gamma_two)
    optical = absorb_part * depth_wet + continuum_part * hot_extinction_thickness
    beam = jnp.exp(-(absorb_part * above_wet + continuum_part * above_warm))
    decay = jnp.exp(-eigen_rate * optical)
    decay_sq = decay * decay
    denominator = eigen_rate + gamma_one + (eigen_rate - gamma_one) * decay_sq
    lost = (gamma_two * (1.0 - decay_sq) + 2.0 * eigen_rate * decay) / denominator
    return beam * (1.0 - lost)


def absorbed_mean(
    depth_wet, hot_extinction_thickness, above_wet, above_warm, absorption, continuum, albedo
):
    band_total = absorption.shape[0]
    band_group = min(8, band_total)
    unit_shape = (1,) * depth_wet.ndim
    running = jnp.zeros_like(depth_wet)
    for band_start in range(0, band_total, band_group):
        absorb_part = absorption[band_start : band_start + band_group].reshape(
            (band_group,) + unit_shape
        )
        continuum_part = continuum[band_start : band_start + band_group].reshape(
            (band_group,) + unit_shape
        )
        reflectivity_share = albedo[band_start : band_start + band_group].reshape(
            (band_group,) + unit_shape
        )
        terms = absorbed_per_band(
            depth_wet[None],
            hot_extinction_thickness[None],
            above_wet[None],
            above_warm[None],
            absorb_part,
            continuum_part,
            reflectivity_share,
        )
        running = running + jnp.sum(terms, axis=0)
    return running / band_total


def local(fields, sl_weights, sl_tile, daylit, absorption, continuum, albedo, wave_ids, legendre):
    meridian_number = lax.axis_size("lon")
    lat_count = lax.axis_size("lat")
    lev_count = lax.axis_size("lev")
    wave_devices = lat_count * meridian_number
    field_count, lev_local, lat_local, lon_local = fields.shape
    tile_width = sl_weights.shape[-1]
    tile_count = lon_local // tile_width
    row_blocks = sl_tile.shape[0]
    block_rows = lat_local // row_blocks
    count = lax.axis_size("lon")
    forward = [(i, (i + 1) % count) for i in range(count)]
    backward = [(target, source) for source, target in forward]
    left = lax.ppermute(fields[..., lon_local - tile_width :], "lon", forward)
    right = lax.ppermute(fields[..., :tile_width], "lon", backward)
    tiles = [left] + [
        fields[..., j * tile_width : (j + 1) * tile_width] for j in range(tile_count)
    ] + [right]
    tile_shape = (field_count, lev_local, row_blocks, block_rows, tile_width)
    outputs = []
    for j in range(tile_count):
        offset = sl_tile[:, j].reshape(1, 1, row_blocks, 1, 1)
        source = jnp.where(
            offset < 0,
            tiles[j].reshape(tile_shape),
            jnp.where(offset > 0, tiles[j + 2].reshape(tile_shape), tiles[j + 1].reshape(tile_shape)),
        )
        outputs.append(
            jnp.einsum("flbrc,btc->bflrt", source, sl_weights[:, j], precision=highest)
        )
    departure_estimate = jnp.concatenate(outputs, axis=-1).transpose(1, 2, 0, 3, 4).reshape(
        field_count, lev_local, lat_local, lon_local
    )
    moisture = departure_estimate[2]
    thermal_state = departure_estimate[0]
    stratum_factor = 4.0 / (lev_local * lev_count)
    depth_wet = stratum_factor * (0.2 + moisture * moisture)
    hot_extinction_thickness = stratum_factor * (0.2 + thermal_state * thermal_state)
    prefix = carried_in(
        jnp.stack([jnp.sum(depth_wet, axis=0), jnp.sum(hot_extinction_thickness, axis=0)]), "lev"
    )
    prefix_wet, prefix_warm = prefix[0], prefix[1]
    wet_levels = []
    warm_levels = []
    for level in range(lev_local):
        wet_levels.append(prefix_wet)
        warm_levels.append(prefix_warm)
        prefix_wet = prefix_wet + depth_wet[level]
        prefix_warm = prefix_warm + hot_extinction_thickness[level]
    above_wet = jnp.stack(wet_levels, axis=0)
    above_warm = jnp.stack(warm_levels, axis=0)
    absorbed = absorbed_mean(
        depth_wet, hot_extinction_thickness, above_wet, above_warm, absorption, continuum, albedo
    )
    absorbed = absorbed.reshape(lev_local, lat_local, tile_count, tile_width)
    heating = (absorbed * daylit.astype(jnp.float32)[None, :, :, None]).reshape(
        lev_local, lat_local, lon_local
    )
    chunk_rows = lev_local * lat_local // meridian_number
    halves = lat_local // chunk_rows

    def to_sectors(block):
        lines = block.reshape(block.shape[0], meridian_number, chunk_rows, lon_local)
        return lax.all_to_all(lines, "lon", split_axis=1, concat_axis=1, tiled=True)

    sectors_rest = to_sectors(departure_estimate[1:])
    sectors_heat = to_sectors(departure_estimate[:1] + heat_rate * heating[None])
    lon_total = lon_local * meridian_number
    wave_total = wave_ids.shape[0]
    inner = jnp.arange(lon_local, dtype=jnp.int32)
    phases = wave_ids[:, None] * inner[None, :] % lon_total
    angles = phases.astype(jnp.float32) * (2.0 * math.pi / lon_total)
    scale = 1.0 / math.sqrt(lon_total)
    dft_table = jnp.concatenate([jnp.cos(angles) * scale, jnp.sin(angles) * scale], axis=0)
    turns = wave_ids[None, :] * jnp.arange(meridian_number, dtype=jnp.int32)[:, None] % meridian_number
    turn_angles = turns.astype(jnp.float32) * (2.0 * math.pi / meridian_number)
    turn_cos = jnp.cos(turn_angles)[:, None, :]
    turn_sin = jnp.sin(turn_angles)[:, None, :]

    def transform(sectors):
        partial = jnp.einsum("fdqn,wn->fdqw", sectors, dft_table, precision=highest)
        cos_part = partial[..., :wave_total]
        sin_part = partial[..., wave_total:]
        real_part = jnp.sum(turn_cos * cos_part - turn_sin * sin_part, axis=1)
        imag_part = -jnp.sum(turn_sin * cos_part + turn_cos * sin_part, axis=1)
        return jnp.stack([real_part, imag_part], axis=1)

    fourier = jnp.concatenate([transform(sectors_heat), transform(sectors_rest)], axis=0)
    waves_local = wave_total // wave_devices
    outgoing_waves = (
        fourier.reshape(field_count, 2, chunk_rows, wave_devices, waves_local)
        .transpose(3, 1, 4, 0, 2)
        .reshape(wave_devices, 2 * waves_local, field_count * chunk_rows)
    )
    arrived = lax.all_to_all(
        outgoing_waves, ("lat", "lon"), split_axis=0, concat_axis=0, tiled=True
    )
    arrived = arrived.reshape(
        lat_count, lev_local, halves, 2, waves_local, field_count, chunk_rows
    )
    spectral_in = arrived.transpose(4, 3, 5, 1, 0, 2, 6).reshape(
        waves_local, 2 * field_count * lev_local, lat_count * lat_local
    )
    lev_here = lax.axis_index("lev")

    def swap(value, flip):
        return lax.ppermute(value, "lev", [(k, k ^ flip) for k in range(lev_count)])

    across = swap(spectral_in, 2)
    by_flip = jnp.stack(
        [spectral_in, swap(spectral_in, 1), across, swap(across, 1)], axis=1
    )
    flipped = jnp.einsum("skqp,snp->skqn", by_flip, legendre, precision=highest)
    flipped = jnp.where((lev_here & 1) == 1, flipped[:, jnp.array([1, 0, 3, 2])], flipped)
    spectra = jnp.where((lev_here & 2) == 2, flipped[:, jnp.array([2, 3, 0, 1])], flipped)
    spectra = (
        spectra.reshape(waves_local, lev_count, 2, field_count, lev_local, -1)
        .transpose(0, 2, 3, 1, 4, 5)
        .reshape(waves_local, 2, field_count, lev_count * lev_local, -1)
    )
    degree_local = legendre.shape[1]
    degrees = lax.axis_index("lev") * degree_local + jnp.arange(degree_local, dtype=jnp.int32)
    own_waves = lax.dynamic_slice_in_dim(
        wave_ids, lax.axis_index(("lat", "lon")) * waves_local, waves_local
    )
    keep_mask = degrees[None, :] >= own_waves[:, None]
    return jnp.where(keep_mask[:, None, None, None, :], spectra, 0.0)


def solution(mesh):
    in_specs = (
        P(None, "lev", "lat", "lon"),
        P("lat", "lon", None, None),
        P("lat", "lon"),
        P("lat", "lon"),
        P(),
        P(),
        P(),
        P(),
        P(("lat", "lon"), "lev", None),
    )
    out_specs = P(("lat", "lon"), None, None, None, "lev")
    return jax.shard_map(local, mesh=mesh, in_specs=in_specs, out_specs=out_specs, check_vma=False)
```

```python
import math

import jax
import jax.numpy as jnp
from jax import lax
from jax.sharding import PartitionSpec as P

highest = lax.Precision.HIGHEST
heat_rate = 6.0
asymmetry = 0.6


def carried_in(planes, axis):
    mine = lax.axis_index(axis)
    pieces = lax.all_gather(planes, axis)
    count = pieces.shape[0]
    below = (jnp.arange(count, dtype=jnp.int32) < mine).reshape((count,) + (1,) * planes.ndim)
    return jnp.sum(jnp.where(below, pieces, 0.0), axis=0)


def absorbed_per_band(
    depth_wet,
    hot_extinction_thickness,
    above_wet,
    above_warm,
    absorb_part,
    continuum_part,
    reflectivity_share,
):
    gamma_one = (7.0 - reflectivity_share * (4.0 + 3.0 * asymmetry)) / 4.0
    gamma_two = -(1.0 - reflectivity_share * (4.0 - 3.0 * asymmetry)) / 4.0
    eigen_rate = jnp.sqrt(gamma_one * gamma_one - gamma_two * gamma_two)
    optical = absorb_part * depth_wet + continuum_part * hot_extinction_thickness
    beam = jnp.exp(-(absorb_part * above_wet + continuum_part * above_warm))
    decay = jnp.exp(-eigen_rate * optical)
    decay_sq = decay * decay
    denominator = eigen_rate + gamma_one + (eigen_rate - gamma_one) * decay_sq
    lost = (gamma_two * (1.0 - decay_sq) + 2.0 * eigen_rate * decay) / denominator
    return beam * (1.0 - lost)


def absorbed_mean(
    depth_wet, hot_extinction_thickness, above_wet, above_warm, absorption, continuum, albedo
):
    band_total = absorption.shape[0]
    band_group = min(8, band_total)
    unit_shape = (1,) * depth_wet.ndim
    running = jnp.zeros_like(depth_wet)
    for band_start in range(0, band_total, band_group):
        absorb_part = absorption[band_start : band_start + band_group].reshape(
            (band_group,) + unit_shape
        )
        continuum_part = continuum[band_start : band_start + band_group].reshape(
            (band_group,) + unit_shape
        )
        reflectivity_share = albedo[band_start : band_start + band_group].reshape(
            (band_group,) + unit_shape
        )
        terms = absorbed_per_band(
            depth_wet[None],
            hot_extinction_thickness[None],
            above_wet[None],
            above_warm[None],
            absorb_part,
            continuum_part,
            reflectivity_share,
        )
        running = running + jnp.sum(terms, axis=0)
    return running / band_total


def local(fields, sl_weights, sl_tile, daylit, absorption, continuum, albedo, wave_ids, legendre):
    meridian_number = lax.axis_size("lon")
    lat_count = lax.axis_size("lat")
    lev_count = lax.axis_size("lev")
    wave_devices = lat_count * meridian_number
    field_count, lev_local, lat_local, lon_local = fields.shape
    tile_width = sl_weights.shape[-1]
    tile_count = lon_local // tile_width
    row_blocks = sl_tile.shape[0]
    block_rows = lat_local // row_blocks
    count = lax.axis_size("lon")
    forward = [(i, (i + 1) % count) for i in range(count)]
    backward = [(target, source) for source, target in forward]
    left = lax.ppermute(fields[..., lon_local - tile_width :], "lon", forward)
    right = lax.ppermute(fields[..., :tile_width], "lon", backward)
    tiles = [left] + [
        fields[..., j * tile_width : (j + 1) * tile_width] for j in range(tile_count)
    ] + [right]
    tile_shape = (field_count, lev_local, row_blocks, block_rows, tile_width)
    outputs = []
    for j in range(tile_count):
        offset = sl_tile[:, j].reshape(1, 1, row_blocks, 1, 1)
        source = jnp.where(
            offset < 0,
            tiles[j].reshape(tile_shape),
            jnp.where(offset > 0, tiles[j + 2].reshape(tile_shape), tiles[j + 1].reshape(tile_shape)),
        )
        outputs.append(
            jnp.einsum("flbrc,btc->bflrt", source, sl_weights[:, j], precision=highest)
        )
    departure_estimate = jnp.concatenate(outputs, axis=-1).transpose(1, 2, 0, 3, 4).reshape(
        field_count, lev_local, lat_local, lon_local
    )
    moisture = departure_estimate[2]
    thermal_state = departure_estimate[0]
    stratum_factor = 4.0 / (lev_local * lev_count)
    depth_wet = stratum_factor * (0.2 + moisture * moisture)
    hot_extinction_thickness = stratum_factor * (0.2 + thermal_state * thermal_state)
    prefix = carried_in(
        jnp.stack([jnp.sum(depth_wet, axis=0), jnp.sum(hot_extinction_thickness, axis=0)]), "lev"
    )
    prefix_wet, prefix_warm = prefix[0], prefix[1]
    wet_levels = []
    warm_levels = []
    for level in range(lev_local):
        wet_levels.append(prefix_wet)
        warm_levels.append(prefix_warm)
        prefix_wet = prefix_wet + depth_wet[level]
        prefix_warm = prefix_warm + hot_extinction_thickness[level]
    above_wet = jnp.stack(wet_levels, axis=0)
    above_warm = jnp.stack(warm_levels, axis=0)
    absorbed = absorbed_mean(
        depth_wet, hot_extinction_thickness, above_wet, above_warm, absorption, continuum, albedo
    )
    absorbed = absorbed.reshape(lev_local, lat_local, tile_count, tile_width)
    heating = (absorbed * daylit.astype(jnp.float32)[None, :, :, None]).reshape(
        lev_local, lat_local, lon_local
    )
    chunk_rows = lev_local * lat_local // meridian_number
    halves = lat_local // chunk_rows

    def to_sectors(block):
        lines = block.reshape(block.shape[0], meridian_number, chunk_rows, lon_local)
        return lax.all_to_all(lines, "lon", split_axis=1, concat_axis=1, tiled=True)

    sectors_rest = to_sectors(departure_estimate[1:])
    sectors_heat = to_sectors(departure_estimate[:1] + heat_rate * heating[None])
    lon_total = lon_local * meridian_number
    wave_total = wave_ids.shape[0]
    inner = jnp.arange(lon_local, dtype=jnp.int32)
    phases = wave_ids[:, None] * inner[None, :] % lon_total
    angles = phases.astype(jnp.float32) * (2.0 * math.pi / lon_total)
    scale = 1.0 / math.sqrt(lon_total)
    dft_table = jnp.concatenate([jnp.cos(angles) * scale, jnp.sin(angles) * scale], axis=0)
    turns = wave_ids[None, :] * jnp.arange(meridian_number, dtype=jnp.int32)[:, None] % meridian_number
    turn_angles = turns.astype(jnp.float32) * (2.0 * math.pi / meridian_number)
    turn_cos = jnp.cos(turn_angles)[:, None, :]
    turn_sin = jnp.sin(turn_angles)[:, None, :]

    def transform(sectors):
        partial = jnp.einsum("fdqn,wn->fdqw", sectors, dft_table, precision=lax.Precision.HIGH)
        cos_part = partial[..., :wave_total]
        sin_part = partial[..., wave_total:]
        real_part = jnp.sum(turn_cos * cos_part - turn_sin * sin_part, axis=1)
        imag_part = -jnp.sum(turn_sin * cos_part + turn_cos * sin_part, axis=1)
        return jnp.stack([real_part, imag_part], axis=1)

    fourier = jnp.concatenate([transform(sectors_heat), transform(sectors_rest)], axis=0)
    waves_local = wave_total // wave_devices
    outgoing_waves = (
        fourier.reshape(field_count, 2, chunk_rows, wave_devices, waves_local)
        .transpose(3, 1, 4, 0, 2)
        .reshape(wave_devices, 2 * waves_local, field_count * chunk_rows)
    )
    arrived = lax.all_to_all(
        outgoing_waves, ("lat", "lon"), split_axis=0, concat_axis=0, tiled=True
    )
    arrived = arrived.reshape(
        lat_count, lev_local, halves, 2, waves_local, field_count, chunk_rows
    )
    spectral_in = arrived.transpose(4, 3, 5, 1, 0, 2, 6).reshape(
        waves_local, 2 * field_count * lev_local, lat_count * lat_local
    )
    lev_here = lax.axis_index("lev")

    def swap(value, flip):
        return lax.ppermute(value, "lev", [(k, k ^ flip) for k in range(lev_count)])

    across = swap(spectral_in, 2)
    by_flip = jnp.stack(
        [spectral_in, swap(spectral_in, 1), across, swap(across, 1)], axis=1
    )
    flipped = jnp.einsum("skqp,snp->skqn", by_flip, legendre, precision=lax.Precision.HIGH)
    flipped = jnp.where((lev_here & 1) == 1, flipped[:, jnp.array([1, 0, 3, 2])], flipped)
    spectra = jnp.where((lev_here & 2) == 2, flipped[:, jnp.array([2, 3, 0, 1])], flipped)
    spectra = (
        spectra.reshape(waves_local, lev_count, 2, field_count, lev_local, -1)
        .transpose(0, 2, 3, 1, 4, 5)
        .reshape(waves_local, 2, field_count, lev_count * lev_local, -1)
    )
    degree_local = legendre.shape[1]
    degrees = lax.axis_index("lev") * degree_local + jnp.arange(degree_local, dtype=jnp.int32)
    own_waves = lax.dynamic_slice_in_dim(
        wave_ids, lax.axis_index(("lat", "lon")) * waves_local, waves_local
    )
    keep_mask = degrees[None, :] >= own_waves[:, None]
    return jnp.where(keep_mask[:, None, None, None, :], spectra, 0.0)


def solution(mesh):
    in_specs = (
        P(None, "lev", "lat", "lon"),
        P("lat", "lon", None, None),
        P("lat", "lon"),
        P("lat", "lon"),
        P(),
        P(),
        P(),
        P(),
        P(("lat", "lon"), "lev", None),
    )
    out_specs = P(("lat", "lon"), None, None, None, "lev")
    return jax.shard_map(local, mesh=mesh, in_specs=in_specs, out_specs=out_specs, check_vma=False)
```

```python
import math

import jax
import jax.numpy as jnp
from jax import lax
from jax.sharding import PartitionSpec as P

highest = lax.Precision.HIGHEST
heat_rate = 6.0
asymmetry = 0.6


def carried_in(planes, axis):
    mine = lax.axis_index(axis)
    pieces = lax.all_gather(planes, axis)
    count = pieces.shape[0]
    below = (jnp.arange(count, dtype=jnp.int32) < mine).reshape((count,) + (1,) * planes.ndim)
    return jnp.sum(jnp.where(below, pieces, 0.0), axis=0)


def absorbed_per_band(
    depth_wet,
    hot_extinction_thickness,
    above_wet,
    above_warm,
    absorb_part,
    continuum_part,
    reflectivity_share,
):
    gamma_one = (7.0 - reflectivity_share * (4.0 + 3.0 * asymmetry)) / 4.0
    gamma_two = -(1.0 - reflectivity_share * (4.0 - 3.0 * asymmetry)) / 4.0
    eigen_rate = jnp.sqrt(gamma_one * gamma_one - gamma_two * gamma_two)
    optical = absorb_part * depth_wet + continuum_part * hot_extinction_thickness
    beam = jnp.exp(-(absorb_part * above_wet + continuum_part * above_warm))
    decay = jnp.exp(-eigen_rate * optical)
    decay_sq = decay * decay
    denominator = eigen_rate + gamma_one + (eigen_rate - gamma_one) * decay_sq
    lost = (gamma_two * (1.0 - decay_sq) + 2.0 * eigen_rate * decay) / denominator
    return beam * (1.0 - lost)


def absorbed_mean(
    depth_wet, hot_extinction_thickness, above_wet, above_warm, absorption, continuum, albedo
):
    band_total = absorption.shape[0]
    band_group = min(8, band_total)
    unit_shape = (1,) * depth_wet.ndim
    running = jnp.zeros_like(depth_wet)
    for band_start in range(0, band_total, band_group):
        absorb_part = absorption[band_start : band_start + band_group].reshape(
            (band_group,) + unit_shape
        )
        continuum_part = continuum[band_start : band_start + band_group].reshape(
            (band_group,) + unit_shape
        )
        reflectivity_share = albedo[band_start : band_start + band_group].reshape(
            (band_group,) + unit_shape
        )
        terms = absorbed_per_band(
            depth_wet[None],
            hot_extinction_thickness[None],
            above_wet[None],
            above_warm[None],
            absorb_part,
            continuum_part,
            reflectivity_share,
        )
        running = running + jnp.sum(terms, axis=0)
    return running / band_total


def local(fields, sl_weights, sl_tile, daylit, absorption, continuum, albedo, wave_ids, legendre):
    meridian_number = lax.axis_size("lon")
    lat_count = lax.axis_size("lat")
    lev_count = lax.axis_size("lev")
    wave_devices = lat_count * meridian_number
    field_count, lev_local, lat_local, lon_local = fields.shape
    tile_width = sl_weights.shape[-1]
    tile_count = lon_local // tile_width
    row_blocks = sl_tile.shape[0]
    block_rows = lat_local // row_blocks
    count = lax.axis_size("lon")
    forward = [(i, (i + 1) % count) for i in range(count)]
    backward = [(target, source) for source, target in forward]
    left = lax.ppermute(fields[..., lon_local - tile_width :], "lon", forward)
    right = lax.ppermute(fields[..., :tile_width], "lon", backward)
    tiles = [left] + [
        fields[..., j * tile_width : (j + 1) * tile_width] for j in range(tile_count)
    ] + [right]
    tile_shape = (field_count, lev_local, row_blocks, block_rows, tile_width)
    outputs = []
    for j in range(tile_count):
        offset = sl_tile[:, j].reshape(1, 1, row_blocks, 1, 1)
        source = jnp.where(
            offset < 0,
            tiles[j].reshape(tile_shape),
            jnp.where(offset > 0, tiles[j + 2].reshape(tile_shape), tiles[j + 1].reshape(tile_shape)),
        )
        outputs.append(
            jnp.einsum("flbrc,btc->bflrt", source, sl_weights[:, j], precision=highest)
        )
    departure_estimate = jnp.concatenate(outputs, axis=-1).transpose(1, 2, 0, 3, 4).reshape(
        field_count, lev_local, lat_local, lon_local
    )
    moisture = departure_estimate[2]
    thermal_state = departure_estimate[0]
    stratum_factor = 4.0 / (lev_local * lev_count)
    depth_wet = stratum_factor * (0.2 + moisture * moisture)
    hot_extinction_thickness = stratum_factor * (0.2 + thermal_state * thermal_state)
    prefix = carried_in(
        jnp.stack([jnp.sum(depth_wet, axis=0), jnp.sum(hot_extinction_thickness, axis=0)]), "lev"
    )
    prefix_wet, prefix_warm = prefix[0], prefix[1]
    wet_levels = []
    warm_levels = []
    for level in range(lev_local):
        wet_levels.append(prefix_wet)
        warm_levels.append(prefix_warm)
        prefix_wet = prefix_wet + depth_wet[level]
        prefix_warm = prefix_warm + hot_extinction_thickness[level]
    above_wet = jnp.stack(wet_levels, axis=0)
    above_warm = jnp.stack(warm_levels, axis=0)
    absorbed = absorbed_mean(
        depth_wet, hot_extinction_thickness, above_wet, above_warm, absorption, continuum, albedo
    )
    absorbed = absorbed.reshape(lev_local, lat_local, tile_count, tile_width)
    heating = (absorbed * daylit.astype(jnp.float32)[None, :, :, None]).reshape(
        lev_local, lat_local, lon_local
    )
    chunk_rows = lev_local * lat_local // meridian_number
    halves = lat_local // chunk_rows

    def to_sectors(block):
        lines = block.reshape(block.shape[0], meridian_number, chunk_rows, lon_local)
        return lax.all_to_all(lines, "lon", split_axis=1, concat_axis=1, tiled=True)

    sectors_rest = to_sectors(departure_estimate[1:])
    sectors_heat = to_sectors(departure_estimate[:1] + heat_rate * heating[None])
    lon_total = lon_local * meridian_number
    wave_total = wave_ids.shape[0]
    inner = jnp.arange(lon_local, dtype=jnp.int32)
    phases = wave_ids[:, None] * inner[None, :] % lon_total
    angles = phases.astype(jnp.float32) * (2.0 * math.pi / lon_total)
    scale = 1.0 / math.sqrt(lon_total)
    dft_table = jnp.concatenate([jnp.cos(angles) * scale, jnp.sin(angles) * scale], axis=0)
    turns = wave_ids[None, :] * jnp.arange(meridian_number, dtype=jnp.int32)[:, None] % meridian_number
    turn_angles = turns.astype(jnp.float32) * (2.0 * math.pi / meridian_number)
    turn_cos = jnp.cos(turn_angles)[:, None, :]
    turn_sin = jnp.sin(turn_angles)[:, None, :]

    def transform(sectors):
        partial = jnp.einsum("fdqn,wn->fdqw", sectors, dft_table, precision=highest)
        cos_part = partial[..., :wave_total]
        sin_part = partial[..., wave_total:]
        real_part = jnp.sum(turn_cos * cos_part - turn_sin * sin_part, axis=1)
        imag_part = -jnp.sum(turn_sin * cos_part + turn_cos * sin_part, axis=1)
        return jnp.stack([real_part, imag_part], axis=1)

    fourier = jnp.concatenate([transform(sectors_heat), transform(sectors_rest)], axis=0)
    waves_local = wave_total // wave_devices
    outgoing_waves = (
        fourier.reshape(field_count, 2, chunk_rows, lat_count, meridian_number, waves_local)
        .transpose(4, 3, 1, 5, 0, 2)
        .reshape(meridian_number, lat_count, 2 * waves_local, field_count * chunk_rows)
    )
    crossed = lax.all_to_all(outgoing_waves, "lon", split_axis=0, concat_axis=0, tiled=True)
    arrived = lax.all_to_all(crossed, "lat", split_axis=1, concat_axis=1, tiled=True)
    arrived = arrived.reshape(
        lev_local, halves, lat_count, 2, waves_local, field_count, chunk_rows
    )
    spectral_in = arrived.transpose(4, 3, 5, 0, 2, 1, 6).reshape(
        waves_local, 2 * field_count * lev_local, lat_count * lat_local
    )
    lev_here = lax.axis_index("lev")

    def swap(value, flip):
        return lax.ppermute(value, "lev", [(k, k ^ flip) for k in range(lev_count)])

    across = swap(spectral_in, 2)
    by_flip = jnp.stack(
        [spectral_in, swap(spectral_in, 1), across, swap(across, 1)], axis=1
    )
    flipped = jnp.einsum("skqp,snp->skqn", by_flip, legendre, precision=highest)
    flipped = jnp.where((lev_here & 1) == 1, flipped[:, jnp.array([1, 0, 3, 2])], flipped)
    spectra = jnp.where((lev_here & 2) == 2, flipped[:, jnp.array([2, 3, 0, 1])], flipped)
    spectra = (
        spectra.reshape(waves_local, lev_count, 2, field_count, lev_local, -1)
        .transpose(0, 2, 3, 1, 4, 5)
        .reshape(waves_local, 2, field_count, lev_count * lev_local, -1)
    )
    degree_local = legendre.shape[1]
    degrees = lax.axis_index("lev") * degree_local + jnp.arange(degree_local, dtype=jnp.int32)
    own_waves = lax.dynamic_slice_in_dim(
        wave_ids, lax.axis_index(("lat", "lon")) * waves_local, waves_local
    )
    keep_mask = degrees[None, :] >= own_waves[:, None]
    return jnp.where(keep_mask[:, None, None, None, :], spectra, 0.0)


def solution(mesh):
    in_specs = (
        P(None, "lev", "lat", "lon"),
        P("lat", "lon", None, None),
        P("lat", "lon"),
        P("lat", "lon"),
        P(),
        P(),
        P(),
        P(),
        P(("lat", "lon"), "lev", None),
    )
    out_specs = P(("lat", "lon"), None, None, None, "lev")
    return jax.shard_map(local, mesh=mesh, in_specs=in_specs, out_specs=out_specs, check_vma=False)
```

```python
import math

import jax
import jax.numpy as jnp
from jax import lax
from jax.sharding import PartitionSpec as P

highest = lax.Precision.HIGHEST
heat_rate = 6.0
asymmetry = 0.6


def carried_in(planes, axis):
    mine = lax.axis_index(axis)
    pieces = lax.all_gather(planes, axis)
    count = pieces.shape[0]
    below = (jnp.arange(count, dtype=jnp.int32) < mine).reshape((count,) + (1,) * planes.ndim)
    return jnp.sum(jnp.where(below, pieces, 0.0), axis=0)


def absorbed_per_band(
    depth_wet,
    hot_extinction_thickness,
    above_wet,
    above_warm,
    absorb_part,
    continuum_part,
    reflectivity_share,
):
    gamma_one = (7.0 - reflectivity_share * (4.0 + 3.0 * asymmetry)) / 4.0
    gamma_two = -(1.0 - reflectivity_share * (4.0 - 3.0 * asymmetry)) / 4.0
    eigen_rate = jnp.sqrt(gamma_one * gamma_one - gamma_two * gamma_two)
    optical = absorb_part * depth_wet + continuum_part * hot_extinction_thickness
    beam = jnp.exp(-(absorb_part * above_wet + continuum_part * above_warm))
    decay = jnp.exp(-eigen_rate * optical)
    decay_sq = decay * decay
    denominator = eigen_rate + gamma_one + (eigen_rate - gamma_one) * decay_sq
    lost = (gamma_two * (1.0 - decay_sq) + 2.0 * eigen_rate * decay) / denominator
    return beam * (1.0 - lost)


def absorbed_mean(
    depth_wet, hot_extinction_thickness, above_wet, above_warm, absorption, continuum, albedo
):
    band_total = absorption.shape[0]
    band_group = min(8, band_total)
    unit_shape = (1,) * depth_wet.ndim
    running = jnp.zeros_like(depth_wet)
    for band_start in range(0, band_total, band_group):
        absorb_part = absorption[band_start : band_start + band_group].reshape(
            (band_group,) + unit_shape
        )
        continuum_part = continuum[band_start : band_start + band_group].reshape(
            (band_group,) + unit_shape
        )
        reflectivity_share = albedo[band_start : band_start + band_group].reshape(
            (band_group,) + unit_shape
        )
        terms = absorbed_per_band(
            depth_wet[None],
            hot_extinction_thickness[None],
            above_wet[None],
            above_warm[None],
            absorb_part,
            continuum_part,
            reflectivity_share,
        )
        running = running + jnp.sum(terms, axis=0)
    return running / band_total


def local(fields, sl_weights, sl_tile, daylit, absorption, continuum, albedo, wave_ids, legendre):
    meridian_number = lax.axis_size("lon")
    lat_count = lax.axis_size("lat")
    lev_count = lax.axis_size("lev")
    wave_devices = lat_count * meridian_number
    field_count, lev_local, lat_local, lon_local = fields.shape
    tile_width = sl_weights.shape[-1]
    tile_count = lon_local // tile_width
    row_blocks = sl_tile.shape[0]
    block_rows = lat_local // row_blocks
    count = lax.axis_size("lon")
    forward = [(i, (i + 1) % count) for i in range(count)]
    backward = [(target, source) for source, target in forward]
    left = lax.ppermute(fields[..., lon_local - tile_width :], "lon", forward)
    right = lax.ppermute(fields[..., :tile_width], "lon", backward)
    tiles = [left] + [
        fields[..., j * tile_width : (j + 1) * tile_width] for j in range(tile_count)
    ] + [right]
    tile_shape = (field_count, lev_local, row_blocks, block_rows, tile_width)
    outputs = []
    for j in range(tile_count):
        offset = sl_tile[:, j].reshape(1, 1, row_blocks, 1, 1)
        source = jnp.where(
            offset < 0,
            tiles[j].reshape(tile_shape),
            jnp.where(offset > 0, tiles[j + 2].reshape(tile_shape), tiles[j + 1].reshape(tile_shape)),
        )
        outputs.append(
            jnp.einsum("flbrc,btc->bflrt", source, sl_weights[:, j], precision=highest)
        )
    departure_estimate = jnp.concatenate(outputs, axis=-1).transpose(1, 2, 0, 3, 4).reshape(
        field_count, lev_local, lat_local, lon_local
    )
    moisture = departure_estimate[2]
    thermal_state = departure_estimate[0]
    stratum_factor = 4.0 / (lev_local * lev_count)
    depth_wet = stratum_factor * (0.2 + moisture * moisture)
    hot_extinction_thickness = stratum_factor * (0.2 + thermal_state * thermal_state)
    prefix = carried_in(
        jnp.stack([jnp.sum(depth_wet, axis=0), jnp.sum(hot_extinction_thickness, axis=0)]), "lev"
    )
    lon_total = lon_local * meridian_number
    wave_total = wave_ids.shape[0]
    inner = jnp.arange(lon_local, dtype=jnp.int32)
    phases = wave_ids[:, None] * inner[None, :] % lon_total
    angles = phases.astype(jnp.float32) * (2.0 * math.pi / lon_total)
    scale = 1.0 / math.sqrt(lon_total)
    dft_table = jnp.concatenate([jnp.cos(angles) * scale, jnp.sin(angles) * scale], axis=0)
    turns = wave_ids[None, :] * jnp.arange(meridian_number, dtype=jnp.int32)[:, None] % meridian_number
    turn_angles = turns.astype(jnp.float32) * (2.0 * math.pi / meridian_number)
    turn_cos = jnp.cos(turn_angles)[:, None, :]
    turn_sin = jnp.sin(turn_angles)[:, None, :]

    prefix, dft_table, turn_cos, turn_sin = lax.optimization_barrier(
        (prefix, dft_table, turn_cos, turn_sin)
    )
    prefix_wet, prefix_warm = prefix[0], prefix[1]
    wet_levels = []
    warm_levels = []
    for level in range(lev_local):
        wet_levels.append(prefix_wet)
        warm_levels.append(prefix_warm)
        prefix_wet = prefix_wet + depth_wet[level]
        prefix_warm = prefix_warm + hot_extinction_thickness[level]
    above_wet = jnp.stack(wet_levels, axis=0)
    above_warm = jnp.stack(warm_levels, axis=0)
    absorbed = absorbed_mean(
        depth_wet, hot_extinction_thickness, above_wet, above_warm, absorption, continuum, albedo
    )
    absorbed = absorbed.reshape(lev_local, lat_local, tile_count, tile_width)
    heating = (absorbed * daylit.astype(jnp.float32)[None, :, :, None]).reshape(
        lev_local, lat_local, lon_local
    )
    chunk_rows = lev_local * lat_local // meridian_number
    halves = lat_local // chunk_rows

    def to_sectors(block):
        lines = block.reshape(block.shape[0], meridian_number, chunk_rows, lon_local)
        return lax.all_to_all(lines, "lon", split_axis=1, concat_axis=1, tiled=True)

    sectors_rest = to_sectors(departure_estimate[1:])
    sectors_heat = to_sectors(departure_estimate[:1] + heat_rate * heating[None])
    def transform(sectors):
        partial = jnp.einsum("fdqn,wn->fdqw", sectors, dft_table, precision=highest)
        cos_part = partial[..., :wave_total]
        sin_part = partial[..., wave_total:]
        real_part = jnp.sum(turn_cos * cos_part - turn_sin * sin_part, axis=1)
        imag_part = -jnp.sum(turn_sin * cos_part + turn_cos * sin_part, axis=1)
        return jnp.stack([real_part, imag_part], axis=1)

    fourier = jnp.concatenate([transform(sectors_heat), transform(sectors_rest)], axis=0)
    waves_local = wave_total // wave_devices
    outgoing_waves = (
        fourier.reshape(field_count, 2, chunk_rows, wave_devices, waves_local)
        .transpose(3, 1, 4, 0, 2)
        .reshape(wave_devices, 2 * waves_local, field_count * chunk_rows)
    )
    arrived = lax.all_to_all(
        outgoing_waves, ("lat", "lon"), split_axis=0, concat_axis=0, tiled=True
    )
    arrived = arrived.reshape(
        lat_count, lev_local, halves, 2, waves_local, field_count, chunk_rows
    )
    spectral_in = arrived.transpose(4, 3, 5, 1, 0, 2, 6).reshape(
        waves_local, 2 * field_count * lev_local, lat_count * lat_local
    )
    lev_here = lax.axis_index("lev")

    def swap(value, flip):
        return lax.ppermute(value, "lev", [(k, k ^ flip) for k in range(lev_count)])

    across = swap(spectral_in, 2)
    by_flip = jnp.stack(
        [spectral_in, swap(spectral_in, 1), across, swap(across, 1)], axis=1
    )
    flipped = jnp.einsum("skqp,snp->skqn", by_flip, legendre, precision=highest)
    flipped = jnp.where((lev_here & 1) == 1, flipped[:, jnp.array([1, 0, 3, 2])], flipped)
    spectra = jnp.where((lev_here & 2) == 2, flipped[:, jnp.array([2, 3, 0, 1])], flipped)
    spectra = (
        spectra.reshape(waves_local, lev_count, 2, field_count, lev_local, -1)
        .transpose(0, 2, 3, 1, 4, 5)
        .reshape(waves_local, 2, field_count, lev_count * lev_local, -1)
    )
    degree_local = legendre.shape[1]
    degrees = lax.axis_index("lev") * degree_local + jnp.arange(degree_local, dtype=jnp.int32)
    own_waves = lax.dynamic_slice_in_dim(
        wave_ids, lax.axis_index(("lat", "lon")) * waves_local, waves_local
    )
    keep_mask = degrees[None, :] >= own_waves[:, None]
    return jnp.where(keep_mask[:, None, None, None, :], spectra, 0.0)


def solution(mesh):
    in_specs = (
        P(None, "lev", "lat", "lon"),
        P("lat", "lon", None, None),
        P("lat", "lon"),
        P("lat", "lon"),
        P(),
        P(),
        P(),
        P(),
        P(("lat", "lon"), "lev", None),
    )
    out_specs = P(("lat", "lon"), None, None, None, "lev")
    return jax.shard_map(local, mesh=mesh, in_specs=in_specs, out_specs=out_specs, check_vma=False)
```

```python
import math

import jax
import jax.numpy as jnp
from jax import lax
from jax.sharding import PartitionSpec as P

highest = lax.Precision.HIGHEST
heat_rate = 6.0
asymmetry = 0.6


def carried_in(planes, axis):
    mine = lax.axis_index(axis)
    pieces = lax.all_gather(planes, axis)
    count = pieces.shape[0]
    below = (jnp.arange(count, dtype=jnp.int32) < mine).reshape((count,) + (1,) * planes.ndim)
    return jnp.sum(jnp.where(below, pieces, 0.0), axis=0)


def absorbed_per_band(
    depth_wet,
    hot_extinction_thickness,
    above_wet,
    above_warm,
    absorb_part,
    continuum_part,
    reflectivity_share,
):
    gamma_one = (7.0 - reflectivity_share * (4.0 + 3.0 * asymmetry)) / 4.0
    gamma_two = -(1.0 - reflectivity_share * (4.0 - 3.0 * asymmetry)) / 4.0
    eigen_rate = jnp.sqrt(gamma_one * gamma_one - gamma_two * gamma_two)
    optical = absorb_part * depth_wet + continuum_part * hot_extinction_thickness
    beam = jnp.exp(-(absorb_part * above_wet + continuum_part * above_warm))
    decay = jnp.exp(-eigen_rate * optical)
    decay_sq = decay * decay
    denominator = eigen_rate + gamma_one + (eigen_rate - gamma_one) * decay_sq
    lost = (gamma_two * (1.0 - decay_sq) + 2.0 * eigen_rate * decay) / denominator
    return beam * (1.0 - lost)


def absorbed_mean(
    depth_wet, hot_extinction_thickness, above_wet, above_warm, absorption, continuum, albedo
):
    band_total = absorption.shape[0]
    band_group = min(8, band_total)
    unit_shape = (1,) * depth_wet.ndim
    running = jnp.zeros_like(depth_wet)
    for band_start in range(0, band_total, band_group):
        absorb_part = absorption[band_start : band_start + band_group].reshape(
            (band_group,) + unit_shape
        )
        continuum_part = continuum[band_start : band_start + band_group].reshape(
            (band_group,) + unit_shape
        )
        reflectivity_share = albedo[band_start : band_start + band_group].reshape(
            (band_group,) + unit_shape
        )
        terms = absorbed_per_band(
            depth_wet[None],
            hot_extinction_thickness[None],
            above_wet[None],
            above_warm[None],
            absorb_part,
            continuum_part,
            reflectivity_share,
        )
        running = running + jnp.sum(terms, axis=0)
    return running / band_total


def local(fields, sl_weights, sl_tile, daylit, absorption, continuum, albedo, wave_ids, legendre):
    meridian_number = lax.axis_size("lon")
    lat_count = lax.axis_size("lat")
    lev_count = lax.axis_size("lev")
    wave_devices = lat_count * meridian_number
    field_count, lev_local, lat_local, lon_local = fields.shape
    tile_width = sl_weights.shape[-1]
    tile_count = lon_local // tile_width
    row_blocks = sl_tile.shape[0]
    block_rows = lat_local // row_blocks
    count = lax.axis_size("lon")
    forward = [(i, (i + 1) % count) for i in range(count)]
    backward = [(target, source) for source, target in forward]
    left = lax.ppermute(fields[..., lon_local - tile_width :], "lon", forward)
    right = lax.ppermute(fields[..., :tile_width], "lon", backward)
    tiles = [left] + [
        fields[..., j * tile_width : (j + 1) * tile_width] for j in range(tile_count)
    ] + [right]
    tile_shape = (field_count, lev_local, row_blocks, block_rows, tile_width)
    outputs = []
    for j in range(tile_count):
        offset = sl_tile[:, j].reshape(1, 1, row_blocks, 1, 1)
        source = jnp.where(
            offset < 0,
            tiles[j].reshape(tile_shape),
            jnp.where(offset > 0, tiles[j + 2].reshape(tile_shape), tiles[j + 1].reshape(tile_shape)),
        )
        outputs.append(
            jnp.einsum("flbrc,btc->bflrt", source, sl_weights[:, j], precision=highest)
        )
    departure_estimate = jnp.concatenate(outputs, axis=-1).transpose(1, 2, 0, 3, 4).reshape(
        field_count, lev_local, lat_local, lon_local
    )
    moisture = departure_estimate[2]
    thermal_state = departure_estimate[0]
    stratum_factor = 4.0 / (lev_local * lev_count)
    depth_wet = stratum_factor * (0.2 + moisture * moisture)
    hot_extinction_thickness = stratum_factor * (0.2 + thermal_state * thermal_state)
    prefix = carried_in(
        jnp.stack([jnp.sum(depth_wet, axis=0), jnp.sum(hot_extinction_thickness, axis=0)]), "lev"
    )
    prefix_wet, prefix_warm = prefix[0], prefix[1]
    wet_levels = []
    warm_levels = []
    for level in range(lev_local):
        wet_levels.append(prefix_wet)
        warm_levels.append(prefix_warm)
        prefix_wet = prefix_wet + depth_wet[level]
        prefix_warm = prefix_warm + hot_extinction_thickness[level]
    above_wet = jnp.stack(wet_levels, axis=0)
    above_warm = jnp.stack(warm_levels, axis=0)
    absorbed = absorbed_mean(
        depth_wet, hot_extinction_thickness, above_wet, above_warm, absorption, continuum, albedo
    )
    absorbed = absorbed.reshape(lev_local, lat_local, tile_count, tile_width)
    heating = (absorbed * daylit.astype(jnp.float32)[None, :, :, None]).reshape(
        lev_local, lat_local, lon_local
    )
    chunk_rows = lev_local * lat_local // meridian_number
    halves = lat_local // chunk_rows

    def to_sectors(block):
        lines = block.reshape(block.shape[0], meridian_number, chunk_rows, lon_local)
        return lax.all_to_all(lines, "lon", split_axis=1, concat_axis=1, tiled=True)

    sectors_rest = to_sectors(departure_estimate[1:])
    sectors_heat = to_sectors(departure_estimate[:1] + heat_rate * heating[None])
    lon_total = lon_local * meridian_number
    wave_total = wave_ids.shape[0]
    inner = jnp.arange(lon_local, dtype=jnp.int32)
    phases = wave_ids[:, None] * inner[None, :] % lon_total
    angles = phases.astype(jnp.float32) * (2.0 * math.pi / lon_total)
    scale = 1.0 / math.sqrt(lon_total)
    dft_table = jnp.concatenate([jnp.cos(angles) * scale, jnp.sin(angles) * scale], axis=0)
    turns = wave_ids[None, :] * jnp.arange(meridian_number, dtype=jnp.int32)[:, None] % meridian_number
    turn_angles = turns.astype(jnp.float32) * (2.0 * math.pi / meridian_number)
    turn_cos = jnp.cos(turn_angles)[:, None, :]
    turn_sin = jnp.sin(turn_angles)[:, None, :]

    def transform(sectors):
        partial = jnp.einsum("fdqn,wn->fdqw", sectors, dft_table, precision=highest)
        cos_part = partial[..., :wave_total]
        sin_part = partial[..., wave_total:]
        real_part = jnp.sum(turn_cos * cos_part - turn_sin * sin_part, axis=1)
        imag_part = -jnp.sum(turn_sin * cos_part + turn_cos * sin_part, axis=1)
        return jnp.stack([real_part, imag_part], axis=1)

    fourier = jnp.concatenate([transform(sectors_heat), transform(sectors_rest)], axis=0)
    waves_local = wave_total // wave_devices
    outgoing_waves = (
        fourier.reshape(field_count, 2, chunk_rows, wave_devices, waves_local)
        .transpose(3, 1, 4, 0, 2)
        .reshape(wave_devices, 2 * waves_local, field_count * chunk_rows)
    )
    arrived = lax.all_to_all(
        outgoing_waves, ("lat", "lon"), split_axis=0, concat_axis=0, tiled=True
    )
    arrived = arrived.reshape(
        lat_count, lev_local, halves, 2, waves_local, field_count, chunk_rows
    )
    spectral_in = arrived.transpose(4, 3, 5, 1, 0, 2, 6).reshape(
        waves_local, 2 * field_count * lev_local, lat_count * lat_local
    )
    lev_here = lax.axis_index("lev")

    def swap(value, flip):
        return lax.ppermute(value, "lev", [(k, k ^ flip) for k in range(lev_count)])

    across = swap(spectral_in, 2)
    by_flip = jnp.stack(
        [spectral_in, swap(spectral_in, 1), across, swap(across, 1)], axis=1
    )
    flipped = jnp.einsum("skqp,snp->skqn", by_flip, legendre, precision=lax.Precision.HIGH)
    flipped = jnp.where((lev_here & 1) == 1, flipped[:, jnp.array([1, 0, 3, 2])], flipped)
    spectra = jnp.where((lev_here & 2) == 2, flipped[:, jnp.array([2, 3, 0, 1])], flipped)
    spectra = (
        spectra.reshape(waves_local, lev_count, 2, field_count, lev_local, -1)
        .transpose(0, 2, 3, 1, 4, 5)
        .reshape(waves_local, 2, field_count, lev_count * lev_local, -1)
    )
    degree_local = legendre.shape[1]
    degrees = lax.axis_index("lev") * degree_local + jnp.arange(degree_local, dtype=jnp.int32)
    own_waves = lax.dynamic_slice_in_dim(
        wave_ids, lax.axis_index(("lat", "lon")) * waves_local, waves_local
    )
    keep_mask = degrees[None, :] >= own_waves[:, None]
    return jnp.where(keep_mask[:, None, None, None, :], spectra, 0.0)


def solution(mesh):
    in_specs = (
        P(None, "lev", "lat", "lon"),
        P("lat", "lon", None, None),
        P("lat", "lon"),
        P("lat", "lon"),
        P(),
        P(),
        P(),
        P(),
        P(("lat", "lon"), "lev", None),
    )
    out_specs = P(("lat", "lon"), None, None, None, "lev")
    return jax.shard_map(local, mesh=mesh, in_specs=in_specs, out_specs=out_specs, check_vma=False)
```

```python
import math

import jax
import jax.numpy as jnp
from jax import lax
from jax.sharding import PartitionSpec as P

highest = lax.Precision.HIGHEST
heat_rate = 6.0
asymmetry = 0.6


def carried_in(planes, axis):
    mine = lax.axis_index(axis)
    pieces = lax.all_gather(planes, axis)
    count = pieces.shape[0]
    below = (jnp.arange(count, dtype=jnp.int32) < mine).reshape((count,) + (1,) * planes.ndim)
    return jnp.sum(jnp.where(below, pieces, 0.0), axis=0)


def absorbed_per_band(
    depth_wet,
    hot_extinction_thickness,
    above_wet,
    above_warm,
    absorb_part,
    continuum_part,
    reflectivity_share,
):
    gamma_one = (7.0 - reflectivity_share * (4.0 + 3.0 * asymmetry)) / 4.0
    gamma_two = -(1.0 - reflectivity_share * (4.0 - 3.0 * asymmetry)) / 4.0
    eigen_rate = jnp.sqrt(gamma_one * gamma_one - gamma_two * gamma_two)
    optical = absorb_part * depth_wet + continuum_part * hot_extinction_thickness
    beam = jnp.exp(-(absorb_part * above_wet + continuum_part * above_warm))
    decay = jnp.exp(-eigen_rate * optical)
    decay_sq = decay * decay
    denominator = eigen_rate + gamma_one + (eigen_rate - gamma_one) * decay_sq
    lost = (gamma_two * (1.0 - decay_sq) + 2.0 * eigen_rate * decay) / denominator
    return beam * (1.0 - lost)


def absorbed_mean(
    depth_wet, hot_extinction_thickness, above_wet, above_warm, absorption, continuum, albedo
):
    band_total = absorption.shape[0]
    band_group = min(8, band_total)
    unit_shape = (1,) * depth_wet.ndim
    running = jnp.zeros_like(depth_wet)
    for band_start in range(0, band_total, band_group):
        absorb_part = absorption[band_start : band_start + band_group].reshape(
            (band_group,) + unit_shape
        )
        continuum_part = continuum[band_start : band_start + band_group].reshape(
            (band_group,) + unit_shape
        )
        reflectivity_share = albedo[band_start : band_start + band_group].reshape(
            (band_group,) + unit_shape
        )
        terms = absorbed_per_band(
            depth_wet[None],
            hot_extinction_thickness[None],
            above_wet[None],
            above_warm[None],
            absorb_part,
            continuum_part,
            reflectivity_share,
        )
        running = running + jnp.sum(terms, axis=0)
    return running / band_total


def local(fields, sl_weights, sl_tile, daylit, absorption, continuum, albedo, wave_ids, legendre):
    meridian_number = lax.axis_size("lon")
    lat_count = lax.axis_size("lat")
    lev_count = lax.axis_size("lev")
    wave_devices = lat_count * meridian_number
    field_count, lev_local, lat_local, lon_local = fields.shape
    tile_width = sl_weights.shape[-1]
    tile_count = lon_local // tile_width
    row_blocks = sl_tile.shape[0]
    block_rows = lat_local // row_blocks
    count = lax.axis_size("lon")
    forward = [(i, (i + 1) % count) for i in range(count)]
    backward = [(target, source) for source, target in forward]
    left = lax.ppermute(fields[..., lon_local - tile_width :], "lon", forward)
    right = lax.ppermute(fields[..., :tile_width], "lon", backward)
    tiles = [left] + [
        fields[..., j * tile_width : (j + 1) * tile_width] for j in range(tile_count)
    ] + [right]
    tile_shape = (field_count, lev_local, row_blocks, block_rows, tile_width)
    outputs = []
    for j in range(tile_count):
        offset = sl_tile[:, j].reshape(1, 1, row_blocks, 1, 1)
        source = jnp.where(
            offset < 0,
            tiles[j].reshape(tile_shape),
            jnp.where(offset > 0, tiles[j + 2].reshape(tile_shape), tiles[j + 1].reshape(tile_shape)),
        )
        outputs.append(
            jnp.einsum("flbrc,btc->bflrt", source, sl_weights[:, j], precision=highest)
        )
    departure_estimate = jnp.concatenate(outputs, axis=-1).transpose(1, 2, 0, 3, 4).reshape(
        field_count, lev_local, lat_local, lon_local
    )
    moisture = departure_estimate[2]
    thermal_state = departure_estimate[0]
    stratum_factor = 4.0 / (lev_local * lev_count)
    depth_wet = stratum_factor * (0.2 + moisture * moisture)
    hot_extinction_thickness = stratum_factor * (0.2 + thermal_state * thermal_state)
    prefix = carried_in(
        jnp.stack([jnp.sum(depth_wet, axis=0), jnp.sum(hot_extinction_thickness, axis=0)]), "lev"
    )
    prefix_wet, prefix_warm = prefix[0], prefix[1]
    wet_levels = []
    warm_levels = []
    for level in range(lev_local):
        wet_levels.append(prefix_wet)
        warm_levels.append(prefix_warm)
        prefix_wet = prefix_wet + depth_wet[level]
        prefix_warm = prefix_warm + hot_extinction_thickness[level]
    above_wet = jnp.stack(wet_levels, axis=0)
    above_warm = jnp.stack(warm_levels, axis=0)
    absorbed = absorbed_mean(
        depth_wet, hot_extinction_thickness, above_wet, above_warm, absorption, continuum, albedo
    )
    absorbed = absorbed.reshape(lev_local, lat_local, tile_count, tile_width)
    heating = (absorbed * daylit.astype(jnp.float32)[None, :, :, None]).reshape(
        lev_local, lat_local, lon_local
    )
    chunk_rows = lev_local * lat_local // meridian_number
    halves = lat_local // chunk_rows

    def to_sectors(block):
        lines = block.reshape(block.shape[0], meridian_number, chunk_rows, lon_local)
        return lax.all_to_all(lines, "lon", split_axis=1, concat_axis=1, tiled=True)

    sectors_rest = to_sectors(departure_estimate[1:])
    sectors_heat = to_sectors(departure_estimate[:1] + heat_rate * heating[None])
    lon_total = lon_local * meridian_number
    wave_total = wave_ids.shape[0]
    inner = jnp.arange(lon_local, dtype=jnp.int32)
    phases = wave_ids[:, None] * inner[None, :] % lon_total
    angles = phases.astype(jnp.float32) * (2.0 * math.pi / lon_total)
    scale = 1.0 / math.sqrt(lon_total)
    dft_table = jnp.concatenate([jnp.cos(angles) * scale, jnp.sin(angles) * scale], axis=0)
    turns = wave_ids[None, :] * jnp.arange(meridian_number, dtype=jnp.int32)[:, None] % meridian_number
    turn_angles = turns.astype(jnp.float32) * (2.0 * math.pi / meridian_number)
    turn_cos = jnp.cos(turn_angles)[:, None, :]
    turn_sin = jnp.sin(turn_angles)[:, None, :]

    def transform(sectors):
        partial = jnp.einsum("fdqn,wn->fdqw", sectors, dft_table, precision=highest)
        cos_part = partial[..., :wave_total]
        sin_part = partial[..., wave_total:]
        real_part = jnp.sum(turn_cos * cos_part - turn_sin * sin_part, axis=1)
        imag_part = -jnp.sum(turn_sin * cos_part + turn_cos * sin_part, axis=1)
        return jnp.stack([real_part, imag_part], axis=1)

    fourier = jnp.concatenate([transform(sectors_heat), transform(sectors_rest)], axis=0)
    waves_local = wave_total // wave_devices
    outgoing_waves = (
        fourier.reshape(field_count, 2, chunk_rows, wave_devices, waves_local)
        .transpose(3, 1, 4, 0, 2)
        .reshape(wave_devices, 2 * waves_local, field_count * chunk_rows)
    )
    arrived = lax.all_to_all(
        outgoing_waves, ("lat", "lon"), split_axis=0, concat_axis=0, tiled=True
    )
    arrived = arrived.reshape(
        lat_count, lev_local, halves, 2, waves_local, field_count, chunk_rows
    )
    spectral_in = arrived.transpose(4, 3, 5, 1, 0, 2, 6).reshape(
        waves_local, 2 * field_count * lev_local, lat_count * lat_local
    )
    lev_here = lax.axis_index("lev")

    def swap(value, flip):
        return lax.ppermute(value, "lev", [(k, k ^ flip) for k in range(lev_count)])

    across = swap(spectral_in, 2)
    by_flip = jnp.concatenate(
        [spectral_in, swap(spectral_in, 1), across, swap(across, 1)], axis=1
    )
    flipped = jnp.einsum("sqp,snp->sqn", by_flip, legendre, precision=highest).reshape(
        waves_local, lev_count, -1, legendre.shape[1]
    )
    flipped = jnp.where((lev_here & 1) == 1, flipped[:, jnp.array([1, 0, 3, 2])], flipped)
    spectra = jnp.where((lev_here & 2) == 2, flipped[:, jnp.array([2, 3, 0, 1])], flipped)
    spectra = (
        spectra.reshape(waves_local, lev_count, 2, field_count, lev_local, -1)
        .transpose(0, 2, 3, 1, 4, 5)
        .reshape(waves_local, 2, field_count, lev_count * lev_local, -1)
    )
    degree_local = legendre.shape[1]
    degrees = lax.axis_index("lev") * degree_local + jnp.arange(degree_local, dtype=jnp.int32)
    own_waves = lax.dynamic_slice_in_dim(
        wave_ids, lax.axis_index(("lat", "lon")) * waves_local, waves_local
    )
    keep_mask = degrees[None, :] >= own_waves[:, None]
    return jnp.where(keep_mask[:, None, None, None, :], spectra, 0.0)


def solution(mesh):
    in_specs = (
        P(None, "lev", "lat", "lon"),
        P("lat", "lon", None, None),
        P("lat", "lon"),
        P("lat", "lon"),
        P(),
        P(),
        P(),
        P(),
        P(("lat", "lon"), "lev", None),
    )
    out_specs = P(("lat", "lon"), None, None, None, "lev")
    return jax.shard_map(local, mesh=mesh, in_specs=in_specs, out_specs=out_specs, check_vma=False)
```
